128 devices in a mesh: dp: 16 (over x, y), head: 8 (over z, core).
Axes of the slice: x: 4, y: 4, z: 4, core: 2. Of those that a mesh axis runs over, the one named last changes fastest.
Arguments:
- tokens: bfloat16 [16384, 2048], P(('dp', 'head')), may hold values from -6 to 6
- cached_lens: int32 [16], replicated, may hold values from 1 to 2048, as said below
- latent_cache: bfloat16 [16, 2048, 576], P(None, 'dp'), may hold values from -720 to 720
- attn_gain: float32 [2048], replicated, may hold values from 0.1 to 1.9
- q_weight: bfloat16 [2048, 3072], P(None, 'head'), may hold values from -0.125 to 0.125
- kv_down: bfloat16 [2048, 576], replicated, may hold values from -0.125 to 0.125
- latent_gain: float32 [512], replicated, may hold values from 0.1 to 1.9
- kv_up: bfloat16 [512, 4096], P(None, 'head'), may hold values from -1 to 1
- o_weight: bfloat16 [2048, 2048], P('head'), may hold values from -0.125 to 0.125
- moe_gain: float32 [2048], replicated, may hold values from 0.1 to 1.9
- routes: int32 [16384, 6], P(('dp', 'head')), may hold values from 0 to 63, all different within a row; in each aligned block of 128 rows (0 to 127, 128 to 255, ...) at most 16 rows name the same one
- route_weights: float32 [16384, 6], P(('dp', 'head')), may hold values from 0.1 to 1
- expert_gate_up: bfloat16 [128, 2048, 1408], P(('dp', 'head')), may hold values from -0.125 to 0.125
- expert_down: bfloat16 [128, 704, 2048], P(('dp', 'head')), may hold values from -0.15625 to 0.15625
Outputs:
- layer_out: bfloat16 [16384, 2048], P(('dp', 'head'))
The draws below stay inside these ranges and needn't reach their ends.
Inputs may be any that keep to these rules, and one draw needn't show every extreme that they name: `cached_lens`: one request's cached length is exactly 2048. `routes`: each token names 6 different experts; among the rows of one device (aligned blocks of 128 tokens) no expert is named more than 16 times, a bound that some block reaches.
All inputs are finite; a program needn't handle non-finite values.
Results may differ from the reference program's by a relative error of at most 0.019.
The reference program's roundings to bfloat16 on the way count: a program that leaves them out, or rounds other values in their place, can miss the bound.
Values may be sent and summed in bfloat16 or wider, within the bound.
No kernel may reach another device: no remote copies, remote signals or barrier semaphores. Data moves between devices by JAX's collectives and lax.ppermute only.
A program may use at most 128 MiB of HBM per device.

```python
import math
import jax
import jax.numpy as jnp
import numpy as np
from jax import lax

D = 2048
HEADS = 16
HN = 128
HR = 64
HV = 128
LAT = 512
FF = 1408
EXPERTS = 64
TOPK = 6
TOK_DEV = 128
CACHE = 2048
SPAN = 1024
REQS = 16
TOKENS = 16384
CAP = 16
HALF = 704
GROUP_HEADS = 2
N_HEAD = 8


def draw_cached_lens(key, part):
    first_key, second_key = jax.random.split(key)
    lengths = jax.random.randint(first_key, (REQS,), 1, CACHE + 1, dtype=jnp.int32)
    chosen = jax.random.randint(second_key, (), 0, REQS, dtype=jnp.int32)
    return jnp.where(jnp.arange(REQS, dtype=jnp.int32) == chosen, CACHE, lengths).astype(jnp.int32)


def draw_latent_cache(key, part):
    key_list = jax.random.split(key, 1)
    values = jnp.clip(jax.random.normal(key_list[0], (REQS, CACHE, LAT + HR), jnp.float32), -6.0, 6.0)
    return values.astype(jnp.bfloat16)


def levels(key, shape, cuts, least, largest):
    gain = 1.0
    for position, parts in cuts:
        steps = jax.random.uniform(jax.random.fold_in(jax.random.fold_in(key, 6), position), (parts,), jnp.float32, least / len(cuts), largest / len(cuts))
        gain = gain * jnp.repeat(jnp.exp(steps), shape[position] // parts).reshape((-1,) + (1,) * (len(shape) - 1 - position))
    return gain


def assign_block(stream_key, own, number, rows, amount, top, bound, skew):
    ranking = jax.random.permutation(stream_key, amount)
    heavy_load, common = portions_of(amount, rows * top, bound, skew, True), portions_of(amount, rows * top, bound, skew, False)
    places = jnp.arange(amount)

    def named(sizes, rotation):
        used = int((sizes > 0).sum())
        fixed = max(1, used // 4)
        moved = fixed + (places - fixed + rotation * (used - fixed)) % max(1, amount - fixed)
        return jnp.zeros((amount,), jnp.int32).at[ranking[jnp.where(places < fixed, places, moved)]].set(jnp.asarray(sizes, jnp.int32))

    sizes = jnp.where(number % 4 == 0, named(heavy_load, number // 4), named(common, number - number // 4 - 1))
    mixed = jax.random.permutation(jax.random.fold_in(own, 3), amount)
    giver, receiver = mixed[0:amount // 2 * 2:2], mixed[1:amount // 2 * 2:2]
    room = jnp.minimum(sizes[giver] - 1, bound - sizes[receiver]) // 2
    room = jnp.where((giver == ranking[0]) | (receiver == ranking[0]) | (sizes[receiver] == 0), 0, jnp.maximum(room, 0))
    moved = jax.random.randint(jax.random.fold_in(own, 4), (amount // 2,), 0, 1 << 20) % (room + 1)
    sizes = sizes.at[giver].add(-moved).at[receiver].add(moved)
    labels = jnp.searchsorted(jnp.cumsum(sizes), jnp.arange(rows * top), side="right").astype(jnp.int32)
    listing = labels.reshape(top, rows).T
    listing = listing[jax.random.permutation(jax.random.fold_in(own, 1), rows)]
    rotation = jax.random.randint(jax.random.fold_in(own, 2), (rows, 1), 0, top)
    return jnp.take_along_axis(listing, (jnp.arange(top)[None, :] + rotation) % top, axis=1)


def portions_of(amount, total, reach, slope, full):
    weights = [(1 << 20) // math.isqrt(grade ** slope) + 1 for grade in range(1, amount + 1)]
    largest = reach if full else min(reach, max(-(-total // amount), total * weights[0] // sum(weights)))
    least = 1 if total - largest >= amount - 1 else 0
    counts, rest = [largest] + [least] * (amount - 1), total - largest - least * (amount - 1)
    while rest > 0:
        candidates = [i for i in range(1, amount) if counts[i] < largest] or [i for i in range(1, amount) if counts[i] < reach]
        whole, remaining = sum([weights[i] for i in candidates]), rest
        for i in candidates:
            addition = min(reach - counts[i], max(1, remaining * weights[i] // whole), rest)
            counts[i] = counts[i] + addition
            rest = rest - addition
    return np.array(counts)


def gaussian(rng, dims, deviation, reach, cuts=(), held_as=jnp.bfloat16):
    result = deviation * jax.random.normal(rng, dims, jnp.float32)
    if cuts:
        result = result * levels(rng, dims, cuts, -0.22, 0.18)
    return jnp.clip(result, -reach, reach).astype(held_as)


def setup_inputs(seed: int = 0) -> dict:
    arg_keys = jax.random.split(jax.random.key(seed), 15)
    tokens = gaussian(arg_keys[0], (TOKENS, D), 1.0, 6.0, ((0, 128),))
    cached_lens = draw_cached_lens(jax.random.fold_in(arg_keys[14], 71), 0)
    latent_cache = draw_latent_cache(jax.random.fold_in(arg_keys[14], 71), 0)
    attn_gain = jnp.clip(1.0 + 0.18 * jax.random.normal(arg_keys[3], (D,), jnp.float32), 0.1, 1.9)
    q_weight = gaussian(arg_keys[4], (D, HEADS * (HN + HR)), D ** -0.5, 0.125, ((1, 8),))
    kv_down = gaussian(arg_keys[5], (D, LAT + HR), D ** -0.5, 0.125)
    latent_gain = jnp.clip(1.0 + 0.18 * jax.random.normal(arg_keys[6], (LAT,), jnp.float32), 0.1, 1.9)
    kv_up = gaussian(arg_keys[7], (LAT, HEADS * (HN + HV)), (LAT // 16) ** -0.5, 1.0, ((1, 8),))
    o_weight = gaussian(arg_keys[8], (HEADS * HV, D), (HEADS * HV) ** -0.5, 0.125, ((0, 8),))
    moe_gain = jnp.clip(1.0 + 0.18 * jax.random.normal(arg_keys[9], (D,), jnp.float32), 0.1, 1.9)
    routes_keys = jax.random.split(jax.random.fold_in(arg_keys[10], 1), TOKENS // TOK_DEV)
    routes_turns = jax.random.permutation(jax.random.fold_in(arg_keys[10], 3), TOKENS // TOK_DEV)
    routes = jax.vmap(lambda own, number: assign_block(jax.random.fold_in(arg_keys[10], 2), own, number, TOK_DEV, EXPERTS, TOPK, CAP, 2))(routes_keys, routes_turns).reshape((TOKENS, TOPK))
    route_weights = jnp.clip(jnp.exp(math.log(1.0) - 2.3025851 * jax.random.uniform(arg_keys[11], (TOKENS, TOPK), jnp.float32) ** levels(arg_keys[11], (TOKENS, TOPK), ((0, 128),), -0.2, 0.2)), 0.1, 1.0)
    expert_gate_up = gaussian(arg_keys[12], (2 * EXPERTS, D, 2 * HALF), D ** -0.5, 0.125, ((0, 128),))
    expert_down = gaussian(arg_keys[13], (2 * EXPERTS, HALF, D), FF ** -0.5, 0.15625, ((0, 128),))
    return {"tokens": tokens, "cached_lens": cached_lens, "latent_cache": latent_cache, "attn_gain": attn_gain, "q_weight": q_weight, "kv_down": kv_down, "latent_gain": latent_gain, "kv_up": kv_up, "o_weight": o_weight, "moe_gain": moe_gain, "routes": routes, "route_weights": route_weights, "expert_gate_up": expert_gate_up, "expert_down": expert_down}


NORM_EPS = 1e-06

def norm_rows(values, gain_row):
    return values * lax.rsqrt(lax.optimization_barrier(jnp.mean(values * values, axis=-1, keepdims=True)) + NORM_EPS) * gain_row

def angle_table(positions):
    half_width = HR // 2
    inverse = np.exp(np.arange(half_width) * (-np.log(10000.0) / half_width)).astype(np.float32)
    return positions.astype(jnp.float32)[:, None] * jnp.asarray(inverse, dtype=jnp.float32)[None, :]

def rotate_pair(values, angles):
    half_width = values.shape[-1] // 2
    cosine = jnp.cos(angles)
    sine_part = jnp.sin(angles)
    former = values[..., :half_width]
    latter = values[..., half_width:]
    return jnp.concatenate([former * cosine - latter * sine_part, latter * cosine + former * sine_part], axis=-1)

def query_rows(normed, q_weight, positions):
    mixed_rows = jnp.dot(normed, q_weight, preferred_element_type=jnp.float32)
    head_count = q_weight.shape[1] // (HN + HR)
    mixed_rows = mixed_rows.reshape(normed.shape[0], head_count, HN + HR)
    turned = rotate_pair(mixed_rows[:, :, HN:], angle_table(positions)[:, None, :])
    joined = jnp.concatenate([mixed_rows[:, :, :HN], turned], axis=2)
    return joined.reshape(normed.shape[0], head_count * (HN + HR)).astype(jnp.bfloat16)

def fresh_rows(normed, kv_down, latent_gain, positions):
    mixed_rows = jnp.dot(normed, kv_down, preferred_element_type=jnp.float32)
    latent = norm_rows(mixed_rows[:, :LAT], latent_gain.astype(jnp.float32))
    turned = rotate_pair(mixed_rows[:, LAT:], angle_table(positions))
    return jnp.concatenate([latent, turned], axis=1).astype(jnp.bfloat16)

def expand_rows(key_rows, kv_up):
    return jnp.dot(key_rows[:, :LAT], kv_up, preferred_element_type=jnp.float32).astype(jnp.bfloat16)

def attend(block_q, key_wide, rope_keys, visible, head_count):
    query_heads = block_q.astype(jnp.float32).reshape(block_q.shape[0], head_count, HN + HR)
    key_heads = key_wide.astype(jnp.float32).reshape(key_wide.shape[0], head_count, HN + HV)
    scores = jnp.einsum('qhd,khd->hqk', query_heads[:, :, :HN], key_heads[:, :, :HN])
    scores = scores + jnp.einsum('qhd,kd->hqk', query_heads[:, :, HN:], rope_keys.astype(jnp.float32))
    scores = scores * (HN + HR) ** (-0.5)
    scores = jnp.where(visible[None], scores, -1e+30)
    row_max = lax.optimization_barrier(jnp.max(scores, axis=2, keepdims=True))
    weights = jnp.where(visible[None], jnp.exp(scores - row_max), 0.0)
    prob_rows = (weights / lax.optimization_barrier(jnp.sum(weights, axis=2, keepdims=True))).astype(jnp.bfloat16)
    mixed_rows = jnp.einsum('hqk,khd->qhd', prob_rows.astype(jnp.float32), key_heads[:, :, HN:])
    return mixed_rows.astype(jnp.bfloat16)

def reference(tokens, cached_lens, latent_cache, attn_gain, q_weight, kv_down, latent_gain, kv_up, o_weight, moe_gain, routes, route_weights, expert_gate_up, expert_down):
    normed = norm_rows(tokens.astype(jnp.float32), attn_gain.astype(jnp.float32)).astype(jnp.bfloat16)
    within = jnp.arange(SPAN, dtype=jnp.int32)
    positions = (cached_lens[:, None] + within[None, :]).reshape(TOKENS)
    queries = query_rows(normed, q_weight, positions)
    fresh_keys = fresh_rows(normed, kv_down, latent_gain, positions)
    block_len = min(512, SPAN)
    key_index = jnp.arange(CACHE + SPAN, dtype=jnp.int32)

    def one_request(request):
        own_queries = lax.dynamic_slice_in_dim(queries, request * SPAN, SPAN, 0)
        own_fresh = lax.dynamic_slice_in_dim(fresh_keys, request * SPAN, SPAN, 0)
        cached_rows = lax.dynamic_index_in_dim(latent_cache, request, 0, keepdims=False)
        key_rows = jnp.concatenate([cached_rows, own_fresh], axis=0)
        key_wide = expand_rows(key_rows, kv_up)
        length = lax.dynamic_index_in_dim(cached_lens, request, 0, keepdims=False)

        def one_block(offset):
            block_q = lax.dynamic_slice_in_dim(own_queries, offset, block_len, 0)
            query_index = offset + jnp.arange(block_len, dtype=jnp.int32)
            visible = jnp.where(key_index[None, :] < CACHE, key_index[None, :] < length, key_index[None, :] - CACHE <= query_index[:, None])
            return attend(block_q, key_wide, key_rows[:, LAT:], visible, HEADS)
        outputs = lax.map(one_block, jnp.arange(0, SPAN, block_len, dtype=jnp.int32))
        return outputs.reshape(SPAN, HEADS * HV)
    heads_out = lax.map(one_request, jnp.arange(REQS, dtype=jnp.int32)).reshape(TOKENS, HEADS * HV)
    group_width = GROUP_HEADS * HV
    attn_out = jnp.zeros((TOKENS, D), jnp.float32)
    for group_index in range(N_HEAD):
        group_term = jnp.dot(heads_out[:, group_index * group_width:(group_index + 1) * group_width], o_weight[group_index * group_width:(group_index + 1) * group_width], preferred_element_type=jnp.float32)
        attn_out = attn_out + lax.optimization_barrier(group_term.astype(jnp.bfloat16)).astype(jnp.float32)
    hidden = tokens.astype(jnp.float32) + attn_out
    moe_in = norm_rows(hidden, moe_gain.astype(jnp.float32)).astype(jnp.bfloat16)
    block_count = TOKENS // TOK_DEV
    pair_count = TOK_DEV * TOPK
    flat_routes = routes.reshape(block_count, pair_count)
    onehot = (flat_routes[:, :, None] == jnp.arange(EXPERTS, dtype=jnp.int32)[None, None, :]).astype(jnp.int32)
    rank_ids = lax.optimization_barrier(jnp.sum((jnp.cumsum(onehot, axis=1) - onehot) * onehot, axis=2))
    block_ids = jnp.arange(block_count, dtype=jnp.int32)[:, None]
    slot_ids = (flat_routes * (block_count * CAP) + block_ids * CAP + rank_ids).reshape(-1)
    token_ids = (block_ids * TOK_DEV + jnp.arange(pair_count, dtype=jnp.int32)[None, :] // TOPK).reshape(-1)
    slot_table = jnp.full((EXPERTS * block_count * CAP,), TOKENS, jnp.int32).at[slot_ids].set(token_ids).reshape(EXPERTS, block_count * CAP)
    weight_table = jnp.zeros((EXPERTS * block_count * CAP,), jnp.float32).at[slot_ids].set(route_weights.reshape(-1)).reshape(EXPERTS, block_count * CAP)
    padded = jnp.concatenate([moe_in, jnp.zeros((1, D), jnp.bfloat16)], axis=0)

    def expert_step(carry_sum, expert):
        row_ids = lax.dynamic_index_in_dim(slot_table, expert, 0, keepdims=False)
        expert_rows = jnp.take(padded, row_ids, axis=0)
        expert_total = jnp.zeros((row_ids.shape[0], D), jnp.float32)
        for half_index in range(2):
            gate_up = lax.dynamic_index_in_dim(expert_gate_up, 2 * expert + half_index, 0, keepdims=False)
            mixed_rows = jnp.dot(expert_rows, gate_up, preferred_element_type=jnp.float32)
            active = (jax.nn.silu(mixed_rows[:, :HALF]) * mixed_rows[:, HALF:]).astype(jnp.bfloat16)
            down_rows = lax.dynamic_index_in_dim(expert_down, 2 * expert + half_index, 0, keepdims=False)
            partial_out = jnp.dot(active, down_rows, preferred_element_type=jnp.float32)
            expert_total = expert_total + lax.optimization_barrier(partial_out.astype(jnp.bfloat16)).astype(jnp.float32)
        scaled = lax.dynamic_index_in_dim(weight_table, expert, 0, keepdims=False)[:, None] * expert_total
        return (carry_sum.at[row_ids].add(scaled, mode='drop'), None)
    routed_out = lax.scan(expert_step, jnp.zeros((TOKENS, D), jnp.float32), jnp.arange(EXPERTS, dtype=jnp.int32))[0]
    return (hidden + routed_out).astype(jnp.bfloat16)
```

```python
import jax
import jax.numpy as jnp
import numpy as np
from jax import lax
from jax.sharding import PartitionSpec as P

D = 2048
HN = 128
HR = 64
HV = 128
LAT = 512
EXPERTS = 64
TOPK = 6
CACHE = 2048
CAP = 16
HALF = 704
HEAD = ("z", "core")
ROWS = ("dp", "z", "core")


NORM_EPS = 1e-06


def norm_rows(values, gain_row):
    return (
        values * lax.rsqrt(jnp.mean(values * values, axis=-1, keepdims=True) + NORM_EPS) * gain_row
    )


def angle_table(positions):
    half_width = HR // 2
    inverse = np.exp(np.arange(half_width) * (-np.log(10000.0) / half_width)).astype(np.float32)
    return positions.astype(jnp.float32)[:, None] * jnp.asarray(inverse, dtype=jnp.float32)[None, :]


def rotate_pair(values, angles):
    half_width = values.shape[-1] // 2
    cosine = jnp.cos(angles)
    sine_part = jnp.sin(angles)
    former = values[..., :half_width]
    latter = values[..., half_width:]
    return jnp.concatenate(
        [former * cosine - latter * sine_part, latter * cosine + former * sine_part], axis=-1
    )


def query_rows(normed, q_weight, positions):
    mixed_rows = jnp.dot(normed, q_weight, preferred_element_type=jnp.float32)
    head_count = q_weight.shape[1] // (HN + HR)
    mixed_rows = mixed_rows.reshape(normed.shape[0], head_count, HN + HR)
    turned = rotate_pair(mixed_rows[:, :, HN:], angle_table(positions)[:, None, :])
    joined = jnp.concatenate([mixed_rows[:, :, :HN], turned], axis=2)
    return joined.reshape(normed.shape[0], head_count * (HN + HR)).astype(jnp.bfloat16)


def fresh_rows(normed, kv_down, latent_gain, positions):
    mixed_rows = jnp.dot(normed, kv_down, preferred_element_type=jnp.float32)
    latent = norm_rows(mixed_rows[:, :LAT], latent_gain)
    turned = rotate_pair(mixed_rows[:, LAT:], angle_table(positions))
    return jnp.concatenate([latent, turned], axis=1).astype(jnp.bfloat16)


def expand_rows(key_rows, kv_up):
    return jnp.dot(key_rows[:, :LAT], kv_up, preferred_element_type=jnp.float32).astype(
        jnp.bfloat16
    )


def attend(block_q, key_wide, rope_keys, visible, head_count):
    query_heads = block_q.reshape(block_q.shape[0], head_count, HN + HR)
    key_heads = key_wide.reshape(key_wide.shape[0], head_count, HN + HV)
    scores = jnp.einsum(
        "qhd,khd->hqk",
        query_heads[:, :, :HN],
        key_heads[:, :, :HN],
        preferred_element_type=jnp.float32,
    )
    scores = scores + jnp.einsum(
        "qhd,kd->hqk", query_heads[:, :, HN:], rope_keys, preferred_element_type=jnp.float32
    )
    scores = scores * (HN + HR) ** (-0.5)
    scores = jnp.where(visible[None], scores, -1e30)
    row_max = jnp.max(scores, axis=2, keepdims=True)
    weights = jnp.where(visible[None], jnp.exp(scores - row_max), 0.0)
    prob_rows = (weights / jnp.sum(weights, axis=2, keepdims=True)).astype(jnp.bfloat16)
    mixed_rows = jnp.einsum(
        "hqk,khd->qhd", prob_rows, key_heads[:, :, HN:], preferred_element_type=jnp.float32
    )
    return mixed_rows.astype(jnp.bfloat16)


def expert_half(rows, gate_up, down):
    mixed_rows = jnp.dot(rows, gate_up, preferred_element_type=jnp.float32)
    active = (jax.nn.silu(mixed_rows[:, :HALF]) * mixed_rows[:, HALF:]).astype(jnp.bfloat16)
    return (
        jnp.dot(active, down, preferred_element_type=jnp.float32)
        .astype(jnp.bfloat16)
        .astype(jnp.float32)
    )


def per_device(
    tokens,
    cached_lens,
    latent_cache,
    attn_gain,
    q_weight,
    kv_down,
    latent_gain,
    kv_up,
    o_weight,
    moe_gain,
    routes,
    route_weights,
    expert_gate_up,
    expert_down,
):
    head_count = lax.axis_size("z") * lax.axis_size("core")
    swap = [(0, 1), (1, 0)]
    other_gate_up = lax.ppermute(expert_gate_up, "core", swap)
    other_down = lax.ppermute(expert_down, "core", swap)
    request = lax.axis_index("dp")
    own_rows = tokens.shape[0]
    span_len = own_rows * head_count
    length = lax.dynamic_index_in_dim(cached_lens, request, 0, keepdims=False)
    local_heads = q_weight.shape[1] // (HN + HR)
    query_width = local_heads * (HN + HR)
    normed = norm_rows(tokens.astype(jnp.float32), attn_gain).astype(jnp.bfloat16)
    shard_rows = lax.all_gather(normed, HEAD, axis=0, tiled=True)
    positions = length + jnp.arange(shard_rows.shape[0], dtype=jnp.int32)
    projected = jnp.concatenate(
        [
            query_rows(shard_rows, q_weight, positions),
            fresh_rows(shard_rows, kv_down, latent_gain, positions),
        ],
        axis=1,
    )
    queries = projected[:, :query_width]
    fresh_keys = projected[:, query_width:]
    owned = lax.all_to_all(latent_cache, "dp", split_axis=0, concat_axis=1, tiled=True)[0]
    key_rows = jnp.concatenate([owned, fresh_keys], axis=0)
    key_wide = expand_rows(key_rows, kv_up)
    rope_keys = key_rows[:, LAT:]
    key_index = jnp.arange(CACHE + span_len, dtype=jnp.int32)
    block_len = min(512, span_len)

    def one_block(offset):
        block_q = lax.dynamic_slice_in_dim(queries, offset, block_len, 0)
        query_index = offset + jnp.arange(block_len, dtype=jnp.int32)
        visible = jnp.where(
            key_index[None, :] < CACHE,
            key_index[None, :] < length,
            key_index[None, :] - CACHE <= query_index[:, None],
        )
        return attend(block_q, key_wide, rope_keys, visible, local_heads)

    heads_out = lax.map(one_block, jnp.arange(0, span_len, block_len, dtype=jnp.int32)).reshape(
        span_len, local_heads * HV
    )
    attn_out = lax.psum_scatter(
        jnp.dot(
            lax.slice_in_dim(heads_out, 0, own_rows * head_count, axis=0),
            o_weight,
            preferred_element_type=jnp.float32,
        ).astype(jnp.bfloat16),
        HEAD,
        scatter_dimension=0,
        tiled=True,
    ).astype(jnp.float32)
    hidden = tokens.astype(jnp.float32) + attn_out
    moe_in = norm_rows(hidden, moe_gain).astype(jnp.bfloat16)
    flat_routes = routes.reshape(-1)
    onehot = (flat_routes[:, None] == jnp.arange(EXPERTS, dtype=jnp.int32)[None, :]).astype(
        jnp.int32
    )
    rank_ids = jnp.sum((jnp.cumsum(onehot, axis=0) - onehot) * onehot, axis=1)
    slot_tk = (flat_routes * CAP + rank_ids).reshape(own_rows, TOPK)
    slot_iota = jnp.arange(EXPERTS * CAP, dtype=jnp.int32)
    dispatch = jnp.any(slot_tk[None, :, :] == slot_iota[:, None, None], axis=2).astype(
        jnp.bfloat16
    )
    outgoing = jnp.dot(dispatch, moe_in, preferred_element_type=jnp.float32).astype(jnp.bfloat16)
    arrived = lax.all_to_all(
        outgoing.reshape(EXPERTS, CAP, D), ("dp", "z"), split_axis=0, concat_axis=0, tiled=True
    ).reshape(EXPERTS * CAP, D)
    total = expert_half(arrived, expert_gate_up[0], expert_down[0]) + expert_half(
        arrived, other_gate_up[0], other_down[0]
    )
    returned = lax.all_to_all(
        total.astype(jnp.bfloat16).reshape(EXPERTS, CAP, D),
        ("dp", "z"),
        split_axis=0,
        concat_axis=0,
        tiled=True,
    ).reshape(EXPERTS * CAP, D)
    routed_out = jnp.zeros((own_rows, D), jnp.float32)
    for k in range(TOPK):
        pick = (slot_tk[:, k : k + 1] == slot_iota[None, :]).astype(jnp.bfloat16)
        chosen = jnp.dot(pick, returned, preferred_element_type=jnp.float32)
        routed_out = routed_out + route_weights[:, k : k + 1] * chosen
    return (hidden + routed_out).astype(jnp.bfloat16)


def solution(mesh):
    chips = jax.sharding.Mesh(
        mesh.devices.reshape(mesh.shape["dp"], -1, 2), ("dp", "z", "core")
    )
    placed = (
        P(ROWS, None),
        P(),
        P(None, "dp", None),
        P(),
        P(None, HEAD),
        P(),
        P(),
        P(None, HEAD),
        P(HEAD, None),
        P(),
        P(ROWS, None),
        P(ROWS, None),
        P(ROWS, None, None),
        P(ROWS, None, None),
    )
    return jax.shard_map(
        per_device, mesh=chips, in_specs=placed, out_specs=P(ROWS, None), check_vma=False
    )
```

```python
import jax
import jax.numpy as jnp
import numpy as np
from jax import lax
from jax.sharding import PartitionSpec as P

D = 2048
HN = 128
HR = 64
HV = 128
LAT = 512
EXPERTS = 64
TOPK = 6
CACHE = 2048
CAP = 16
HALF = 704
HEAD = ("z", "core")
ROWS = ("dp", "z", "core")


NORM_EPS = 1e-06


def norm_rows(values, gain_row):
    return (
        values * lax.rsqrt(jnp.mean(values * values, axis=-1, keepdims=True) + NORM_EPS) * gain_row
    )


def angle_table(positions):
    half_width = HR // 2
    inverse = np.exp(np.arange(half_width) * (-np.log(10000.0) / half_width)).astype(np.float32)
    return positions.astype(jnp.float32)[:, None] * jnp.asarray(inverse, dtype=jnp.float32)[None, :]


def rotate_pair(values, angles):
    half_width = values.shape[-1] // 2
    cosine = jnp.cos(angles)
    sine_part = jnp.sin(angles)
    former = values[..., :half_width]
    latter = values[..., half_width:]
    return jnp.concatenate(
        [former * cosine - latter * sine_part, latter * cosine + former * sine_part], axis=-1
    )


def query_rows(normed, q_weight, positions):
    mixed_rows = jnp.dot(normed, q_weight, preferred_element_type=jnp.float32)
    head_count = q_weight.shape[1] // (HN + HR)
    mixed_rows = mixed_rows.reshape(normed.shape[0], head_count, HN + HR)
    turned = rotate_pair(mixed_rows[:, :, HN:], angle_table(positions)[:, None, :])
    joined = jnp.concatenate([mixed_rows[:, :, :HN], turned], axis=2)
    return joined.reshape(normed.shape[0], head_count * (HN + HR)).astype(jnp.bfloat16)


def fresh_rows(normed, kv_down, latent_gain, positions):
    mixed_rows = jnp.dot(normed, kv_down, preferred_element_type=jnp.float32)
    latent = norm_rows(mixed_rows[:, :LAT], latent_gain)
    turned = rotate_pair(mixed_rows[:, LAT:], angle_table(positions))
    return jnp.concatenate([latent, turned], axis=1).astype(jnp.bfloat16)


def expand_rows(key_rows, kv_up):
    return jnp.dot(key_rows[:, :LAT], kv_up, preferred_element_type=jnp.float32).astype(
        jnp.bfloat16
    )


def attend(block_q, key_wide, rope_keys, visible, head_count):
    query_heads = block_q.reshape(block_q.shape[0], head_count, HN + HR)
    key_heads = key_wide.reshape(key_wide.shape[0], head_count, HN + HV)
    scores = jnp.einsum(
        "qhd,khd->hqk",
        query_heads[:, :, :HN],
        key_heads[:, :, :HN],
        preferred_element_type=jnp.float32,
    )
    scores = scores + jnp.einsum(
        "qhd,kd->hqk", query_heads[:, :, HN:], rope_keys, preferred_element_type=jnp.float32
    )
    scores = scores * (HN + HR) ** (-0.5)
    scores = jnp.where(visible[None], scores, -1e30)
    row_max = jnp.max(scores, axis=2, keepdims=True)
    weights = jnp.where(visible[None], jnp.exp(scores - row_max), 0.0)
    prob_rows = (weights / jnp.sum(weights, axis=2, keepdims=True)).astype(jnp.bfloat16)
    mixed_rows = jnp.einsum(
        "hqk,khd->qhd", prob_rows, key_heads[:, :, HN:], preferred_element_type=jnp.float32
    )
    return mixed_rows.astype(jnp.bfloat16)


def expert_half(rows, gate_up, down):
    mixed_rows = jnp.dot(rows, gate_up, preferred_element_type=jnp.float32)
    active = (jax.nn.silu(mixed_rows[:, :HALF]) * mixed_rows[:, HALF:]).astype(jnp.bfloat16)
    return (
        jnp.dot(active, down, preferred_element_type=jnp.float32)
        .astype(jnp.bfloat16)
        .astype(jnp.float32)
    )


def per_device(
    tokens,
    cached_lens,
    latent_cache,
    attn_gain,
    q_weight,
    kv_down,
    latent_gain,
    kv_up,
    o_weight,
    moe_gain,
    routes,
    route_weights,
    expert_gate_up,
    expert_down,
):
    head_count = lax.axis_size("z") * lax.axis_size("core")
    swap = [(0, 1), (1, 0)]
    other_gate_up = lax.ppermute(expert_gate_up, "core", swap)
    other_down = lax.ppermute(expert_down, "core", swap)
    request = lax.axis_index("dp")
    own_rows = tokens.shape[0]
    span_len = own_rows * head_count
    length = lax.dynamic_index_in_dim(cached_lens, request, 0, keepdims=False)
    local_heads = q_weight.shape[1] // (HN + HR)
    query_width = local_heads * (HN + HR)
    normed = norm_rows(tokens.astype(jnp.float32), attn_gain).astype(jnp.bfloat16)
    shard_rows = lax.all_gather(normed, HEAD, axis=0, tiled=True)
    o_src, shard_rows = lax.optimization_barrier((o_weight, shard_rows))
    o_full = lax.all_gather(o_src, HEAD, axis=0, tiled=True)
    positions = length + jnp.arange(shard_rows.shape[0], dtype=jnp.int32)
    projected = jnp.concatenate(
        [
            query_rows(shard_rows, q_weight, positions),
            fresh_rows(shard_rows, kv_down, latent_gain, positions),
        ],
        axis=1,
    )
    queries = projected[:, :query_width]
    fresh_keys = projected[:, query_width:]
    core = lax.axis_index("core")
    quarter = latent_cache.shape[1] // 2
    mine = lax.all_to_all(
        lax.dynamic_slice_in_dim(latent_cache, core * quarter, quarter, 1),
        "dp",
        split_axis=0,
        concat_axis=1,
        tiled=True,
    )[0]
    theirs = lax.ppermute(mine, "core", swap)
    cache_rows = jnp.arange(mine.shape[0], dtype=jnp.int32)
    cache_pos = cache_rows // quarter * (2 * quarter) + cache_rows % quarter
    key_rows = jnp.concatenate([mine, theirs, fresh_keys], axis=0)
    key_wide = expand_rows(key_rows, kv_up)
    rope_keys = key_rows[:, LAT:]
    key_index = jnp.concatenate(
        [
            cache_pos + core * quarter,
            cache_pos + (1 - core) * quarter,
            CACHE + jnp.arange(span_len, dtype=jnp.int32),
        ]
    )
    block_len = min(512, span_len)

    def one_block(offset):
        block_q = lax.dynamic_slice_in_dim(queries, offset, block_len, 0)
        query_index = offset + jnp.arange(block_len, dtype=jnp.int32)
        visible = jnp.where(
            key_index[None, :] < CACHE,
            key_index[None, :] < length,
            key_index[None, :] - CACHE <= query_index[:, None],
        )
        return attend(block_q, key_wide, rope_keys, visible, local_heads)

    heads_out = lax.map(one_block, jnp.arange(0, span_len, block_len, dtype=jnp.int32)).reshape(
        span_len, local_heads * HV
    )
    heads_mine = lax.all_to_all(heads_out, HEAD, split_axis=0, concat_axis=1, tiled=True)
    group_terms = jnp.einsum(
        "tgc,gcd->gtd",
        heads_mine.reshape(own_rows, head_count, -1),
        o_full.reshape(head_count, -1, D),
        preferred_element_type=jnp.float32,
    )
    attn_out = jnp.sum(group_terms.astype(jnp.bfloat16).astype(jnp.float32), axis=0)
    hidden = tokens.astype(jnp.float32) + attn_out
    moe_in = norm_rows(hidden, moe_gain).astype(jnp.bfloat16)
    flat_routes = routes.reshape(-1)
    onehot = (flat_routes[:, None] == jnp.arange(EXPERTS, dtype=jnp.int32)[None, :]).astype(
        jnp.int32
    )
    rank_ids = jnp.sum((jnp.cumsum(onehot, axis=0) - onehot) * onehot, axis=1)
    slot_tk = (flat_routes * CAP + rank_ids).reshape(own_rows, TOPK)
    slot_iota = jnp.arange(EXPERTS * CAP, dtype=jnp.int32)
    dispatch = jnp.any(slot_tk[None, :, :] == slot_iota[:, None, None], axis=2).astype(
        jnp.bfloat16
    )
    outgoing = jnp.dot(dispatch, moe_in, preferred_element_type=jnp.float32).astype(jnp.bfloat16)
    arrived = lax.all_to_all(
        outgoing.reshape(EXPERTS, CAP, D), ("dp", "z"), split_axis=0, concat_axis=0, tiled=True
    ).reshape(EXPERTS * CAP, D)
    total = expert_half(arrived, expert_gate_up[0], expert_down[0]) + expert_half(
        arrived, other_gate_up[0], other_down[0]
    )
    returned = lax.all_to_all(
        total.astype(jnp.bfloat16).reshape(EXPERTS, CAP, D),
        ("dp", "z"),
        split_axis=0,
        concat_axis=0,
        tiled=True,
    ).reshape(EXPERTS * CAP, D)
    routed_out = jnp.zeros((own_rows, D), jnp.float32)
    for k in range(TOPK):
        pick = (slot_tk[:, k : k + 1] == slot_iota[None, :]).astype(jnp.bfloat16)
        chosen = jnp.dot(pick, returned, preferred_element_type=jnp.float32)
        routed_out = routed_out + route_weights[:, k : k + 1] * chosen
    return (hidden + routed_out).astype(jnp.bfloat16)


def solution(mesh):
    chips = jax.sharding.Mesh(
        mesh.devices.reshape(mesh.shape["dp"], -1, 2), ("dp", "z", "core")
    )
    placed = (
        P(ROWS, None),
        P(),
        P(None, "dp", None),
        P(),
        P(None, HEAD),
        P(),
        P(),
        P(None, HEAD),
        P(HEAD, None),
        P(),
        P(ROWS, None),
        P(ROWS, None),
        P(ROWS, None, None),
        P(ROWS, None, None),
    )
    return jax.shard_map(
        per_device, mesh=chips, in_specs=placed, out_specs=P(ROWS, None), check_vma=False
    )
```

```python
import jax
import jax.numpy as jnp
import numpy as np
from jax import lax
from jax.experimental import pallas as pl
from jax.experimental.pallas import tpu as pltpu
from jax.sharding import PartitionSpec as P

D = 2048
HN = 128
HR = 64
HV = 128
LAT = 512
EXPERTS = 64
TOPK = 6
CACHE = 2048
CAP = 16
HALF = 704
HEAD = ("z", "core")
ROWS = ("dp", "z", "core")


NORM_EPS = 1e-06


def norm_rows(values, gain_row):
    return (
        values * lax.rsqrt(jnp.mean(values * values, axis=-1, keepdims=True) + NORM_EPS) * gain_row
    )


def angle_table(positions):
    half_width = HR // 2
    inverse = np.exp(np.arange(half_width) * (-np.log(10000.0) / half_width)).astype(np.float32)
    return positions.astype(jnp.float32)[:, None] * jnp.asarray(inverse, dtype=jnp.float32)[None, :]


def rotate_pair(values, angles):
    half_width = values.shape[-1] // 2
    cosine = jnp.cos(angles)
    sine_part = jnp.sin(angles)
    former = values[..., :half_width]
    latter = values[..., half_width:]
    return jnp.concatenate(
        [former * cosine - latter * sine_part, latter * cosine + former * sine_part], axis=-1
    )


def query_rows(normed, q_weight, positions):
    mixed_rows = jnp.dot(normed, q_weight, preferred_element_type=jnp.float32)
    head_count = q_weight.shape[1] // (HN + HR)
    mixed_rows = mixed_rows.reshape(normed.shape[0], head_count, HN + HR)
    turned = rotate_pair(mixed_rows[:, :, HN:], angle_table(positions)[:, None, :])
    joined = jnp.concatenate([mixed_rows[:, :, :HN], turned], axis=2)
    return joined.reshape(normed.shape[0], head_count * (HN + HR)).astype(jnp.bfloat16)


def fresh_rows(normed, kv_down, latent_gain, positions):
    mixed_rows = jnp.dot(normed, kv_down, preferred_element_type=jnp.float32)
    latent = norm_rows(mixed_rows[:, :LAT], latent_gain)
    turned = rotate_pair(mixed_rows[:, LAT:], angle_table(positions))
    return jnp.concatenate([latent, turned], axis=1).astype(jnp.bfloat16)


def expand_rows(key_rows, kv_up):
    return jnp.dot(key_rows[:, :LAT], kv_up, preferred_element_type=jnp.float32).astype(
        jnp.bfloat16
    )


def attend(block_q, key_wide, rope_keys, visible, head_count):
    query_heads = block_q.reshape(block_q.shape[0], head_count, HN + HR)
    key_heads = key_wide.reshape(key_wide.shape[0], head_count, HN + HV)
    scores = jnp.einsum(
        "qhd,khd->hqk",
        query_heads[:, :, :HN],
        key_heads[:, :, :HN],
        preferred_element_type=jnp.float32,
    )
    scores = scores + jnp.einsum(
        "qhd,kd->hqk", query_heads[:, :, HN:], rope_keys, preferred_element_type=jnp.float32
    )
    scores = scores * (HN + HR) ** (-0.5)
    scores = jnp.where(visible[None], scores, -1e30)
    row_max = jnp.max(scores, axis=2, keepdims=True)
    weights = jnp.where(visible[None], jnp.exp(scores - row_max), 0.0)
    prob_rows = (weights / jnp.sum(weights, axis=2, keepdims=True)).astype(jnp.bfloat16)
    mixed_rows = jnp.einsum(
        "hqk,khd->qhd", prob_rows, key_heads[:, :, HN:], preferred_element_type=jnp.float32
    )
    return mixed_rows.astype(jnp.bfloat16)


Q_BLOCK = 256


def attend_kernel(qn_ref, qr_ref, kw_ref, kr_ref, th_ref, o_ref):
    heads = qr_ref.shape[0]
    first = pl.program_id(0) * Q_BLOCK
    q_idx = first + lax.broadcasted_iota(jnp.int32, (Q_BLOCK, 1), 0)
    visible = q_idx >= th_ref[...]
    kr = kr_ref[...]
    contract = (((1,), (1,)), ((), ()))
    for h in range(heads):
        qn = qn_ref[:, h * HN : (h + 1) * HN]
        kn = kw_ref[:, h * (HN + HV) : h * (HN + HV) + HN]
        vals = kw_ref[:, h * (HN + HV) + HN : (h + 1) * (HN + HV)]
        scores = lax.dot_general(qn, kn, contract, preferred_element_type=jnp.float32)
        scores = scores + lax.dot_general(
            qr_ref[h], kr, contract, preferred_element_type=jnp.float32
        )
        scores = scores * (HN + HR) ** (-0.5)
        scores = jnp.where(visible, scores, -1e30)
        row_max = jnp.max(scores, axis=1, keepdims=True)
        weights = jnp.where(visible, jnp.exp(scores - row_max), 0.0)
        prob_rows = (weights / jnp.sum(weights, axis=1, keepdims=True)).astype(jnp.bfloat16)
        mixed = jnp.dot(prob_rows, vals, preferred_element_type=jnp.float32)
        o_ref[:, h * HV : (h + 1) * HV] = mixed.astype(jnp.bfloat16)


def attend_all(q_nope, q_rope, key_wide, rope_keys, thresh, interpret=False):
    span, nope_width = q_nope.shape
    heads = q_rope.shape[0]
    keys = key_wide.shape[0]
    return pl.pallas_call(
        attend_kernel,
        grid=(span // Q_BLOCK,),
        in_specs=[
            pl.BlockSpec((Q_BLOCK, nope_width), lambda i: (i, 0)),
            pl.BlockSpec((heads, Q_BLOCK, HR), lambda i: (0, i, 0)),
            pl.BlockSpec((keys, key_wide.shape[1]), lambda i: (0, 0)),
            pl.BlockSpec((keys, HR), lambda i: (0, 0)),
            pl.BlockSpec((1, keys), lambda i: (0, 0)),
        ],
        out_specs=pl.BlockSpec((Q_BLOCK, heads * HV), lambda i: (i, 0)),
        out_shape=jax.ShapeDtypeStruct((span, heads * HV), jnp.bfloat16),
        compiler_params=pltpu.CompilerParams(
            dimension_semantics=("arbitrary",), vmem_limit_bytes=48 * 1024 * 1024
        ),
        interpret=interpret,
    )(q_nope, q_rope, key_wide, rope_keys, thresh)


def expert_half(rows, gate_up, down):
    mixed_rows = jnp.dot(rows, gate_up, preferred_element_type=jnp.float32)
    active = (jax.nn.silu(mixed_rows[:, :HALF]) * mixed_rows[:, HALF:]).astype(jnp.bfloat16)
    return (
        jnp.dot(active, down, preferred_element_type=jnp.float32)
        .astype(jnp.bfloat16)
        .astype(jnp.float32)
    )


def per_device(
    tokens,
    cached_lens,
    latent_cache,
    attn_gain,
    q_weight,
    kv_down,
    latent_gain,
    kv_up,
    o_weight,
    moe_gain,
    routes,
    route_weights,
    expert_gate_up,
    expert_down,
):
    head_count = lax.axis_size("z") * lax.axis_size("core")
    swap = [(0, 1), (1, 0)]
    other_gate_up = lax.ppermute(expert_gate_up, "core", swap)
    other_down = lax.ppermute(expert_down, "core", swap)
    request = lax.axis_index("dp")
    own_rows = tokens.shape[0]
    span_len = own_rows * head_count
    length = lax.dynamic_index_in_dim(cached_lens, request, 0, keepdims=False)
    local_heads = q_weight.shape[1] // (HN + HR)
    query_width = local_heads * (HN + HR)
    normed = norm_rows(tokens.astype(jnp.float32), attn_gain).astype(jnp.bfloat16)
    shard_rows = lax.all_gather(normed, HEAD, axis=0, tiled=True)
    o_src, shard_rows = lax.optimization_barrier((o_weight, shard_rows))
    o_full = lax.all_gather(o_src, HEAD, axis=0, tiled=True)
    positions = length + jnp.arange(shard_rows.shape[0], dtype=jnp.int32)
    projected = jnp.concatenate(
        [
            query_rows(shard_rows, q_weight, positions),
            fresh_rows(shard_rows, kv_down, latent_gain, positions),
        ],
        axis=1,
    )
    queries = projected[:, :query_width]
    fresh_keys = projected[:, query_width:]
    core = lax.axis_index("core")
    quarter = latent_cache.shape[1] // 2
    mine = lax.all_to_all(
        lax.dynamic_slice_in_dim(latent_cache, core * quarter, quarter, 1),
        "dp",
        split_axis=0,
        concat_axis=1,
        tiled=True,
    )[0]
    theirs = lax.ppermute(mine, "core", swap)
    cache_rows = jnp.arange(mine.shape[0], dtype=jnp.int32)
    cache_pos = cache_rows // quarter * (2 * quarter) + cache_rows % quarter
    key_rows = jnp.concatenate([mine, theirs, fresh_keys], axis=0)
    key_wide = expand_rows(key_rows, kv_up)
    rope_keys = key_rows[:, LAT:]
    key_index = jnp.concatenate(
        [
            cache_pos + core * quarter,
            cache_pos + (1 - core) * quarter,
            CACHE + jnp.arange(span_len, dtype=jnp.int32),
        ]
    )
    thresh = jnp.where(
        key_index < CACHE, jnp.where(key_index < length, -1, 1 << 30), key_index - CACHE
    ).reshape(1, -1)
    query_heads = queries.reshape(span_len, local_heads, HN + HR)
    heads_out = attend_all(
        query_heads[:, :, :HN].reshape(span_len, local_heads * HN),
        query_heads[:, :, HN:].transpose(1, 0, 2),
        key_wide,
        rope_keys,
        thresh,
    )
    heads_mine = lax.all_to_all(heads_out, HEAD, split_axis=0, concat_axis=1, tiled=True)
    group_terms = jnp.einsum(
        "tgc,gcd->gtd",
        heads_mine.reshape(own_rows, head_count, -1),
        o_full.reshape(head_count, -1, D),
        preferred_element_type=jnp.float32,
    )
    attn_out = jnp.sum(group_terms.astype(jnp.bfloat16).astype(jnp.float32), axis=0)
    hidden = tokens.astype(jnp.float32) + attn_out
    moe_in = norm_rows(hidden, moe_gain).astype(jnp.bfloat16)
    flat_routes = routes.reshape(-1)
    onehot = (flat_routes[:, None] == jnp.arange(EXPERTS, dtype=jnp.int32)[None, :]).astype(
        jnp.int32
    )
    rank_ids = jnp.sum((jnp.cumsum(onehot, axis=0) - onehot) * onehot, axis=1)
    slot_tk = (flat_routes * CAP + rank_ids).reshape(own_rows, TOPK)
    slot_iota = jnp.arange(EXPERTS * CAP, dtype=jnp.int32)
    dispatch = jnp.any(slot_tk[None, :, :] == slot_iota[:, None, None], axis=2).astype(
        jnp.bfloat16
    )
    outgoing = jnp.dot(dispatch, moe_in, preferred_element_type=jnp.float32).astype(jnp.bfloat16)
    arrived = lax.all_to_all(
        outgoing.reshape(EXPERTS, CAP, D), ("dp", "z"), split_axis=0, concat_axis=0, tiled=True
    ).reshape(EXPERTS * CAP, D)
    total = expert_half(arrived, expert_gate_up[0], expert_down[0]) + expert_half(
        arrived, other_gate_up[0], other_down[0]
    )
    returned = lax.all_to_all(
        total.astype(jnp.bfloat16).reshape(EXPERTS, CAP, D),
        ("dp", "z"),
        split_axis=0,
        concat_axis=0,
        tiled=True,
    ).reshape(EXPERTS * CAP, D)
    routed_out = jnp.zeros((own_rows, D), jnp.float32)
    for k in range(TOPK):
        pick = (slot_tk[:, k : k + 1] == slot_iota[None, :]).astype(jnp.bfloat16)
        chosen = jnp.dot(pick, returned, preferred_element_type=jnp.float32)
        routed_out = routed_out + route_weights[:, k : k + 1] * chosen
    return (hidden + routed_out).astype(jnp.bfloat16)


def solution(mesh):
    chips = jax.sharding.Mesh(
        mesh.devices.reshape(mesh.shape["dp"], -1, 2), ("dp", "z", "core")
    )
    placed = (
        P(ROWS, None),
        P(),
        P(None, "dp", None),
        P(),
        P(None, HEAD),
        P(),
        P(),
        P(None, HEAD),
        P(HEAD, None),
        P(),
        P(ROWS, None),
        P(ROWS, None),
        P(ROWS, None, None),
        P(ROWS, None, None),
    )
    return jax.shard_map(
        per_device, mesh=chips, in_specs=placed, out_specs=P(ROWS, None), check_vma=False
    )
```

```python
import jax
import jax.numpy as jnp
import numpy as np
from jax import lax
from jax.experimental import pallas as pl
from jax.experimental.pallas import tpu as pltpu
from jax.sharding import PartitionSpec as P

D = 2048
HN = 128
HR = 64
HV = 128
LAT = 512
EXPERTS = 64
TOPK = 6
CACHE = 2048
CAP = 16
HALF = 704
HEAD = ("z", "core")
ROWS = ("dp", "z", "core")


NORM_EPS = 1e-06


def norm_rows(values, gain_row):
    return (
        values * lax.rsqrt(jnp.mean(values * values, axis=-1, keepdims=True) + NORM_EPS) * gain_row
    )


def angle_table(positions):
    half_width = HR // 2
    inverse = np.exp(np.arange(half_width) * (-np.log(10000.0) / half_width)).astype(np.float32)
    return positions.astype(jnp.float32)[:, None] * jnp.asarray(inverse, dtype=jnp.float32)[None, :]


def rotate_pair(values, angles):
    half_width = values.shape[-1] // 2
    cosine = jnp.cos(angles)
    sine_part = jnp.sin(angles)
    former = values[..., :half_width]
    latter = values[..., half_width:]
    return jnp.concatenate(
        [former * cosine - latter * sine_part, latter * cosine + former * sine_part], axis=-1
    )


def query_rows(normed, q_weight, positions):
    mixed_rows = jnp.dot(normed, q_weight, preferred_element_type=jnp.float32)
    head_count = q_weight.shape[1] // (HN + HR)
    mixed_rows = mixed_rows.reshape(normed.shape[0], head_count, HN + HR)
    turned = rotate_pair(mixed_rows[:, :, HN:], angle_table(positions)[:, None, :])
    joined = jnp.concatenate([mixed_rows[:, :, :HN], turned], axis=2)
    return joined.reshape(normed.shape[0], head_count * (HN + HR)).astype(jnp.bfloat16)


def fresh_rows(normed, kv_down, latent_gain, positions):
    mixed_rows = jnp.dot(normed, kv_down, preferred_element_type=jnp.float32)
    latent = norm_rows(mixed_rows[:, :LAT], latent_gain)
    turned = rotate_pair(mixed_rows[:, LAT:], angle_table(positions))
    return jnp.concatenate([latent, turned], axis=1).astype(jnp.bfloat16)


def expand_rows(key_rows, kv_up):
    return jnp.dot(key_rows[:, :LAT], kv_up, preferred_element_type=jnp.float32).astype(
        jnp.bfloat16
    )


def attend(block_q, key_wide, rope_keys, visible, head_count):
    query_heads = block_q.reshape(block_q.shape[0], head_count, HN + HR)
    key_heads = key_wide.reshape(key_wide.shape[0], head_count, HN + HV)
    scores = jnp.einsum(
        "qhd,khd->hqk",
        query_heads[:, :, :HN],
        key_heads[:, :, :HN],
        preferred_element_type=jnp.float32,
    )
    scores = scores + jnp.einsum(
        "qhd,kd->hqk", query_heads[:, :, HN:], rope_keys, preferred_element_type=jnp.float32
    )
    scores = scores * (HN + HR) ** (-0.5)
    scores = jnp.where(visible[None], scores, -1e30)
    row_max = jnp.max(scores, axis=2, keepdims=True)
    weights = jnp.where(visible[None], jnp.exp(scores - row_max), 0.0)
    prob_rows = (weights / jnp.sum(weights, axis=2, keepdims=True)).astype(jnp.bfloat16)
    mixed_rows = jnp.einsum(
        "hqk,khd->qhd", prob_rows, key_heads[:, :, HN:], preferred_element_type=jnp.float32
    )
    return mixed_rows.astype(jnp.bfloat16)


Q_BLOCK = 256


def attend_kernel(qn_ref, qr_ref, kw_ref, kr_ref, th_ref, tq_ref, o_ref):
    heads = qr_ref.shape[0]
    visible = tq_ref[...] >= th_ref[...]
    kr = kr_ref[...]
    contract = (((1,), (1,)), ((), ()))
    for h in range(heads):
        qn = qn_ref[:, h * HN : (h + 1) * HN]
        kn = kw_ref[:, h * (HN + HV) : h * (HN + HV) + HN]
        vals = kw_ref[:, h * (HN + HV) + HN : (h + 1) * (HN + HV)]
        scores = lax.dot_general(qn, kn, contract, preferred_element_type=jnp.float32)
        scores = scores + lax.dot_general(
            qr_ref[h], kr, contract, preferred_element_type=jnp.float32
        )
        scores = scores * (HN + HR) ** (-0.5)
        scores = jnp.where(visible, scores, -1e30)
        row_max = jnp.max(scores, axis=1, keepdims=True)
        weights = jnp.where(visible, jnp.exp(scores - row_max), 0.0)
        prob_rows = (weights / jnp.sum(weights, axis=1, keepdims=True)).astype(jnp.bfloat16)
        mixed = jnp.dot(prob_rows, vals, preferred_element_type=jnp.float32)
        o_ref[:, h * HV : (h + 1) * HV] = mixed.astype(jnp.bfloat16)


def attend_all(q_nope, q_rope, key_wide, rope_keys, thresh, q_tokens, interpret=False):
    span, nope_width = q_nope.shape
    heads = q_rope.shape[0]
    keys = key_wide.shape[0]
    return pl.pallas_call(
        attend_kernel,
        grid=(span // Q_BLOCK,),
        in_specs=[
            pl.BlockSpec((Q_BLOCK, nope_width), lambda i: (i, 0)),
            pl.BlockSpec((heads, Q_BLOCK, HR), lambda i: (0, i, 0)),
            pl.BlockSpec((keys, key_wide.shape[1]), lambda i: (0, 0)),
            pl.BlockSpec((keys, HR), lambda i: (0, 0)),
            pl.BlockSpec((1, keys), lambda i: (0, 0)),
            pl.BlockSpec((Q_BLOCK, 1), lambda i: (i, 0)),
        ],
        out_specs=pl.BlockSpec((Q_BLOCK, heads * HV), lambda i: (i, 0)),
        out_shape=jax.ShapeDtypeStruct((span, heads * HV), jnp.bfloat16),
        compiler_params=pltpu.CompilerParams(
            dimension_semantics=("arbitrary",), vmem_limit_bytes=48 * 1024 * 1024
        ),
        interpret=interpret,
    )(q_nope, q_rope, key_wide, rope_keys, thresh, q_tokens)


def expert_half(rows, gate_up, down):
    mixed_rows = jnp.dot(rows, gate_up, preferred_element_type=jnp.float32)
    active = (jax.nn.silu(mixed_rows[:, :HALF]) * mixed_rows[:, HALF:]).astype(jnp.bfloat16)
    return (
        jnp.dot(active, down, preferred_element_type=jnp.float32)
        .astype(jnp.bfloat16)
        .astype(jnp.float32)
    )


def per_device(
    tokens,
    cached_lens,
    latent_cache,
    attn_gain,
    q_weight,
    kv_down,
    latent_gain,
    kv_up,
    o_weight,
    moe_gain,
    routes,
    route_weights,
    expert_gate_up,
    expert_down,
):
    head_count = lax.axis_size("z") * lax.axis_size("core")
    swap = [(0, 1), (1, 0)]
    other_gate_up = lax.ppermute(expert_gate_up, "core", swap)
    other_down = lax.ppermute(expert_down, "core", swap)
    request = lax.axis_index("dp")
    own_rows = tokens.shape[0]
    span_len = own_rows * head_count
    length = lax.dynamic_index_in_dim(cached_lens, request, 0, keepdims=False)
    local_heads = q_weight.shape[1] // (HN + HR)
    query_width = local_heads * (HN + HR)
    normed = norm_rows(tokens.astype(jnp.float32), attn_gain).astype(jnp.bfloat16)
    z_count = lax.axis_size("z")
    shard_rows = lax.all_gather(
        lax.all_gather(normed, "z", axis=0, tiled=True), "core", axis=0, tiled=True
    )
    o_src, shard_rows = lax.optimization_barrier((o_weight, shard_rows))
    o_full = lax.all_gather(
        lax.all_gather(o_src, "z", axis=0, tiled=True), "core", axis=0, tiled=True
    )
    row_ids = jnp.arange(span_len, dtype=jnp.int32)
    token_of_row = (
        (row_ids // own_rows % z_count) * (head_count // z_count) + row_ids // (own_rows * z_count)
    ) * own_rows + row_ids % own_rows
    positions = length + token_of_row
    projected = jnp.concatenate(
        [
            query_rows(shard_rows, q_weight, positions),
            fresh_rows(shard_rows, kv_down, latent_gain, positions),
        ],
        axis=1,
    )
    queries = projected[:, :query_width]
    fresh_keys = projected[:, query_width:]
    core = lax.axis_index("core")
    quarter = latent_cache.shape[1] // 2
    mine = lax.all_to_all(
        lax.dynamic_slice_in_dim(latent_cache, core * quarter, quarter, 1),
        "dp",
        split_axis=0,
        concat_axis=1,
        tiled=True,
    )[0]
    theirs = lax.ppermute(mine, "core", swap)
    cache_rows = jnp.arange(mine.shape[0], dtype=jnp.int32)
    cache_pos = cache_rows // quarter * (2 * quarter) + cache_rows % quarter
    key_rows = jnp.concatenate([mine, theirs, fresh_keys], axis=0)
    key_wide = expand_rows(key_rows, kv_up)
    rope_keys = key_rows[:, LAT:]
    key_index = jnp.concatenate(
        [
            cache_pos + core * quarter,
            cache_pos + (1 - core) * quarter,
            CACHE + token_of_row,
        ]
    )
    thresh = jnp.where(
        key_index < CACHE, jnp.where(key_index < length, -1, 1 << 30), key_index - CACHE
    ).reshape(1, -1)
    query_heads = queries.reshape(span_len, local_heads, HN + HR)
    heads_out = attend_all(
        query_heads[:, :, :HN].reshape(span_len, local_heads * HN),
        query_heads[:, :, HN:].transpose(1, 0, 2),
        key_wide,
        rope_keys,
        thresh,
        token_of_row.reshape(-1, 1),
    )
    heads_mine = lax.all_to_all(
        heads_out, ("core", "z"), split_axis=0, concat_axis=1, tiled=True
    )
    group_terms = jnp.einsum(
        "tgc,gcd->gtd",
        heads_mine.reshape(own_rows, head_count, -1),
        o_full.reshape(head_count, -1, D),
        preferred_element_type=jnp.float32,
    )
    attn_out = jnp.sum(group_terms.astype(jnp.bfloat16).astype(jnp.float32), axis=0)
    hidden = tokens.astype(jnp.float32) + attn_out
    moe_in = norm_rows(hidden, moe_gain).astype(jnp.bfloat16)
    flat_routes = routes.reshape(-1)
    onehot = (flat_routes[:, None] == jnp.arange(EXPERTS, dtype=jnp.int32)[None, :]).astype(
        jnp.int32
    )
    rank_ids = jnp.sum((jnp.cumsum(onehot, axis=0) - onehot) * onehot, axis=1)
    slot_tk = (flat_routes * CAP + rank_ids).reshape(own_rows, TOPK)
    slot_iota = jnp.arange(EXPERTS * CAP, dtype=jnp.int32)
    dispatch = jnp.any(slot_tk[None, :, :] == slot_iota[:, None, None], axis=2).astype(
        jnp.bfloat16
    )
    outgoing = jnp.dot(dispatch, moe_in, preferred_element_type=jnp.float32).astype(jnp.bfloat16)
    arrived = lax.all_to_all(
        outgoing.reshape(EXPERTS, CAP, D), ("dp", "z"), split_axis=0, concat_axis=0, tiled=True
    ).reshape(EXPERTS * CAP, D)
    total = expert_half(arrived, expert_gate_up[0], expert_down[0]) + expert_half(
        arrived, other_gate_up[0], other_down[0]
    )
    returned = lax.all_to_all(
        total.astype(jnp.bfloat16).reshape(EXPERTS, CAP, D),
        ("dp", "z"),
        split_axis=0,
        concat_axis=0,
        tiled=True,
    ).reshape(EXPERTS * CAP, D)
    slot_weights = jnp.sum(
        jnp.where(slot_tk[:, :, None] == slot_iota[None, None, :], route_weights[:, :, None], 0.0),
        axis=1,
    )
    weights_hi = slot_weights.astype(jnp.bfloat16)
    weights_lo = (slot_weights - weights_hi.astype(jnp.float32)).astype(jnp.bfloat16)
    routed_out = jnp.dot(weights_hi, returned, preferred_element_type=jnp.float32) + jnp.dot(
        weights_lo, returned, preferred_element_type=jnp.float32
    )
    return (hidden + routed_out).astype(jnp.bfloat16)


def solution(mesh):
    chips = jax.sharding.Mesh(
        mesh.devices.reshape(mesh.shape["dp"], -1, 2), ("dp", "z", "core")
    )
    placed = (
        P(ROWS, None),
        P(),
        P(None, "dp", None),
        P(),
        P(None, HEAD),
        P(),
        P(),
        P(None, HEAD),
        P(HEAD, None),
        P(),
        P(ROWS, None),
        P(ROWS, None),
        P(ROWS, None, None),
        P(ROWS, None, None),
    )
    return jax.shard_map(
        per_device, mesh=chips, in_specs=placed, out_specs=P(ROWS, None), check_vma=False
    )
```

```python
import jax
import jax.numpy as jnp
import numpy as np
from jax import lax
from jax.experimental import pallas as pl
from jax.experimental.pallas import tpu as pltpu
from jax.sharding import PartitionSpec as P

D = 2048
HN = 128
HR = 64
HV = 128
LAT = 512
EXPERTS = 64
TOPK = 6
CACHE = 2048
CAP = 16
HALF = 704
HEAD = ("z", "core")
ROWS = ("dp", "z", "core")


NORM_EPS = 1e-06


def norm_rows(values, gain_row):
    return (
        values * lax.rsqrt(jnp.mean(values * values, axis=-1, keepdims=True) + NORM_EPS) * gain_row
    )


def angle_table(positions):
    half_width = HR // 2
    inverse = np.exp(np.arange(half_width) * (-np.log(10000.0) / half_width)).astype(np.float32)
    return positions.astype(jnp.float32)[:, None] * jnp.asarray(inverse, dtype=jnp.float32)[None, :]


def rotate_pair(values, angles):
    half_width = values.shape[-1] // 2
    cosine = jnp.cos(angles)
    sine_part = jnp.sin(angles)
    former = values[..., :half_width]
    latter = values[..., half_width:]
    return jnp.concatenate(
        [former * cosine - latter * sine_part, latter * cosine + former * sine_part], axis=-1
    )


def query_rows(normed, q_weight, positions):
    mixed_rows = jnp.dot(normed, q_weight, preferred_element_type=jnp.float32)
    head_count = q_weight.shape[1] // (HN + HR)
    mixed_rows = mixed_rows.reshape(normed.shape[0], head_count, HN + HR)
    turned = rotate_pair(mixed_rows[:, :, HN:], angle_table(positions)[:, None, :])
    joined = jnp.concatenate([mixed_rows[:, :, :HN], turned], axis=2)
    return joined.reshape(normed.shape[0], head_count * (HN + HR)).astype(jnp.bfloat16)


def fresh_rows(normed, kv_down, latent_gain, positions):
    mixed_rows = jnp.dot(normed, kv_down, preferred_element_type=jnp.float32)
    latent = norm_rows(mixed_rows[:, :LAT], latent_gain)
    turned = rotate_pair(mixed_rows[:, LAT:], angle_table(positions))
    return jnp.concatenate([latent, turned], axis=1).astype(jnp.bfloat16)


def expand_rows(key_rows, kv_up):
    return jnp.dot(key_rows[:, :LAT], kv_up, preferred_element_type=jnp.float32).astype(
        jnp.bfloat16
    )


def attend(block_q, key_wide, rope_keys, visible, head_count):
    query_heads = block_q.reshape(block_q.shape[0], head_count, HN + HR)
    key_heads = key_wide.reshape(key_wide.shape[0], head_count, HN + HV)
    scores = jnp.einsum(
        "qhd,khd->hqk",
        query_heads[:, :, :HN],
        key_heads[:, :, :HN],
        preferred_element_type=jnp.float32,
    )
    scores = scores + jnp.einsum(
        "qhd,kd->hqk", query_heads[:, :, HN:], rope_keys, preferred_element_type=jnp.float32
    )
    scores = scores * (HN + HR) ** (-0.5)
    scores = jnp.where(visible[None], scores, -1e30)
    row_max = jnp.max(scores, axis=2, keepdims=True)
    weights = jnp.where(visible[None], jnp.exp(scores - row_max), 0.0)
    prob_rows = (weights / jnp.sum(weights, axis=2, keepdims=True)).astype(jnp.bfloat16)
    mixed_rows = jnp.einsum(
        "hqk,khd->qhd", prob_rows, key_heads[:, :, HN:], preferred_element_type=jnp.float32
    )
    return mixed_rows.astype(jnp.bfloat16)


Q_BLOCK = 256


def attend_kernel(qn_ref, qr_ref, kw_ref, kr_ref, th_ref, o_ref):
    heads = qr_ref.shape[0]
    first = pl.program_id(0) * Q_BLOCK
    q_idx = first + lax.broadcasted_iota(jnp.int32, (Q_BLOCK, 1), 0)
    visible = q_idx >= th_ref[...]
    kr = kr_ref[...]
    contract = (((1,), (1,)), ((), ()))
    for h in range(heads):
        qn = qn_ref[:, h * HN : (h + 1) * HN]
        kn = kw_ref[:, h * (HN + HV) : h * (HN + HV) + HN]
        vals = kw_ref[:, h * (HN + HV) + HN : (h + 1) * (HN + HV)]
        scores = lax.dot_general(qn, kn, contract, preferred_element_type=jnp.float32)
        scores = scores + lax.dot_general(
            qr_ref[h], kr, contract, preferred_element_type=jnp.float32
        )
        scores = scores * (HN + HR) ** (-0.5)
        scores = jnp.where(visible, scores, -1e30)
        row_max = jnp.max(scores, axis=1, keepdims=True)
        weights = jnp.where(visible, jnp.exp(scores - row_max), 0.0)
        prob_rows = (weights / jnp.sum(weights, axis=1, keepdims=True)).astype(jnp.bfloat16)
        mixed = jnp.dot(prob_rows, vals, preferred_element_type=jnp.float32)
        o_ref[:, h * HV : (h + 1) * HV] = mixed.astype(jnp.bfloat16)


def attend_all(q_nope, q_rope, key_wide, rope_keys, thresh, interpret=False):
    span, nope_width = q_nope.shape
    heads = q_rope.shape[0]
    keys = key_wide.shape[0]
    return pl.pallas_call(
        attend_kernel,
        grid=(span // Q_BLOCK,),
        in_specs=[
            pl.BlockSpec((Q_BLOCK, nope_width), lambda i: (i, 0)),
            pl.BlockSpec((heads, Q_BLOCK, HR), lambda i: (0, i, 0)),
            pl.BlockSpec((keys, key_wide.shape[1]), lambda i: (0, 0)),
            pl.BlockSpec((keys, HR), lambda i: (0, 0)),
            pl.BlockSpec((1, keys), lambda i: (0, 0)),
        ],
        out_specs=pl.BlockSpec((Q_BLOCK, heads * HV), lambda i: (i, 0)),
        out_shape=jax.ShapeDtypeStruct((span, heads * HV), jnp.bfloat16),
        compiler_params=pltpu.CompilerParams(
            dimension_semantics=("arbitrary",), vmem_limit_bytes=48 * 1024 * 1024
        ),
        interpret=interpret,
    )(q_nope, q_rope, key_wide, rope_keys, thresh)


def expert_half(rows, gate_up, down):
    mixed_rows = jnp.dot(rows, gate_up, preferred_element_type=jnp.float32)
    active = (jax.nn.silu(mixed_rows[:, :HALF]) * mixed_rows[:, HALF:]).astype(jnp.bfloat16)
    return (
        jnp.dot(active, down, preferred_element_type=jnp.float32)
        .astype(jnp.bfloat16)
        .astype(jnp.float32)
    )


def per_device(
    tokens,
    cached_lens,
    latent_cache,
    attn_gain,
    q_weight,
    kv_down,
    latent_gain,
    kv_up,
    o_weight,
    moe_gain,
    routes,
    route_weights,
    expert_gate_up,
    expert_down,
):
    head_count = lax.axis_size("z") * lax.axis_size("core")
    swap = [(0, 1), (1, 0)]
    other_gate_up = lax.ppermute(expert_gate_up, "core", swap)
    other_down = lax.ppermute(expert_down, "core", swap)
    request = lax.axis_index("dp")
    own_rows = tokens.shape[0]
    span_len = own_rows * head_count
    length = lax.dynamic_index_in_dim(cached_lens, request, 0, keepdims=False)
    local_heads = q_weight.shape[1] // (HN + HR)
    query_width = local_heads * (HN + HR)
    normed = norm_rows(tokens.astype(jnp.float32), attn_gain).astype(jnp.bfloat16)
    shard_rows = lax.all_to_all(
        jnp.broadcast_to(normed, (head_count,) + normed.shape),
        HEAD,
        split_axis=0,
        concat_axis=0,
        tiled=True,
    ).reshape(head_count * own_rows, D)
    o_src, shard_rows = lax.optimization_barrier((o_weight, shard_rows))
    o_full = lax.all_gather(o_src, HEAD, axis=0, tiled=True)
    positions = length + jnp.arange(shard_rows.shape[0], dtype=jnp.int32)
    projected = jnp.concatenate(
        [
            query_rows(shard_rows, q_weight, positions),
            fresh_rows(shard_rows, kv_down, latent_gain, positions),
        ],
        axis=1,
    )
    queries = projected[:, :query_width]
    fresh_keys = projected[:, query_width:]
    core = lax.axis_index("core")
    quarter = latent_cache.shape[1] // 2
    mine = lax.all_to_all(
        lax.dynamic_slice_in_dim(latent_cache, core * quarter, quarter, 1),
        "dp",
        split_axis=0,
        concat_axis=1,
        tiled=True,
    )[0]
    theirs = lax.ppermute(mine, "core", swap)
    cache_rows = jnp.arange(mine.shape[0], dtype=jnp.int32)
    cache_pos = cache_rows // quarter * (2 * quarter) + cache_rows % quarter
    key_rows = jnp.concatenate([mine, theirs, fresh_keys], axis=0)
    key_wide = expand_rows(key_rows, kv_up)
    rope_keys = key_rows[:, LAT:]
    key_index = jnp.concatenate(
        [
            cache_pos + core * quarter,
            cache_pos + (1 - core) * quarter,
            CACHE + jnp.arange(span_len, dtype=jnp.int32),
        ]
    )
    thresh = jnp.where(
        key_index < CACHE, jnp.where(key_index < length, -1, 1 << 30), key_index - CACHE
    ).reshape(1, -1)
    query_heads = queries.reshape(span_len, local_heads, HN + HR)
    heads_out = attend_all(
        query_heads[:, :, :HN].reshape(span_len, local_heads * HN),
        query_heads[:, :, HN:].transpose(1, 0, 2),
        key_wide,
        rope_keys,
        thresh,
    )
    heads_mine = lax.all_to_all(heads_out, HEAD, split_axis=0, concat_axis=1, tiled=True)
    group_terms = jnp.einsum(
        "tgc,gcd->gtd",
        heads_mine.reshape(own_rows, head_count, -1),
        o_full.reshape(head_count, -1, D),
        preferred_element_type=jnp.float32,
    )
    attn_out = jnp.sum(group_terms.astype(jnp.bfloat16).astype(jnp.float32), axis=0)
    hidden = tokens.astype(jnp.float32) + attn_out
    moe_in = norm_rows(hidden, moe_gain).astype(jnp.bfloat16)
    flat_routes = routes.reshape(-1)
    onehot = (flat_routes[:, None] == jnp.arange(EXPERTS, dtype=jnp.int32)[None, :]).astype(
        jnp.int32
    )
    rank_ids = jnp.sum((jnp.cumsum(onehot, axis=0) - onehot) * onehot, axis=1)
    slot_tk = (flat_routes * CAP + rank_ids).reshape(own_rows, TOPK)
    slot_iota = jnp.arange(EXPERTS * CAP, dtype=jnp.int32)
    dispatch = jnp.any(slot_tk[None, :, :] == slot_iota[:, None, None], axis=2).astype(
        jnp.bfloat16
    )
    outgoing = jnp.dot(dispatch, moe_in, preferred_element_type=jnp.float32).astype(jnp.bfloat16)
    arrived = lax.all_to_all(
        outgoing.reshape(EXPERTS, CAP, D), ("dp", "z"), split_axis=0, concat_axis=0, tiled=True
    ).reshape(EXPERTS * CAP, D)
    total = expert_half(arrived, expert_gate_up[0], expert_down[0]) + expert_half(
        arrived, other_gate_up[0], other_down[0]
    )
    returned = lax.all_to_all(
        total.astype(jnp.bfloat16).reshape(EXPERTS, CAP, D),
        ("dp", "z"),
        split_axis=0,
        concat_axis=0,
        tiled=True,
    ).reshape(EXPERTS * CAP, D)
    slot_weights = jnp.sum(
        jnp.where(slot_tk[:, :, None] == slot_iota[None, None, :], route_weights[:, :, None], 0.0),
        axis=1,
    )
    weights_hi = slot_weights.astype(jnp.bfloat16)
    weights_lo = (slot_weights - weights_hi.astype(jnp.float32)).astype(jnp.bfloat16)
    routed_out = jnp.dot(weights_hi, returned, preferred_element_type=jnp.float32) + jnp.dot(
        weights_lo, returned, preferred_element_type=jnp.float32
    )
    return (hidden + routed_out).astype(jnp.bfloat16)


def solution(mesh):
    chips = jax.sharding.Mesh(
        mesh.devices.reshape(mesh.shape["dp"], -1, 2), ("dp", "z", "core")
    )
    placed = (
        P(ROWS, None),
        P(),
        P(None, "dp", None),
        P(),
        P(None, HEAD),
        P(),
        P(),
        P(None, HEAD),
        P(HEAD, None),
        P(),
        P(ROWS, None),
        P(ROWS, None),
        P(ROWS, None, None),
        P(ROWS, None, None),
    )
    return jax.shard_map(
        per_device, mesh=chips, in_specs=placed, out_specs=P(ROWS, None), check_vma=False
    )
```

```python
import jax
import jax.numpy as jnp
import numpy as np
from jax import lax
from jax.experimental import pallas as pl
from jax.experimental.pallas import tpu as pltpu
from jax.sharding import PartitionSpec as P

D = 2048
HN = 128
HR = 64
HV = 128
LAT = 512
EXPERTS = 64
TOPK = 6
CACHE = 2048
CAP = 16
HALF = 704
HEAD = ("z", "core")
ROWS = ("dp", "z", "core")


NORM_EPS = 1e-06


def norm_rows(values, gain_row):
    return (
        values * lax.rsqrt(jnp.mean(values * values, axis=-1, keepdims=True) + NORM_EPS) * gain_row
    )


def angle_table(positions):
    half_width = HR // 2
    inverse = np.exp(np.arange(half_width) * (-np.log(10000.0) / half_width)).astype(np.float32)
    return positions.astype(jnp.float32)[:, None] * jnp.asarray(inverse, dtype=jnp.float32)[None, :]


def rotate_pair(values, angles):
    half_width = values.shape[-1] // 2
    cosine = jnp.cos(angles)
    sine_part = jnp.sin(angles)
    former = values[..., :half_width]
    latter = values[..., half_width:]
    return jnp.concatenate(
        [former * cosine - latter * sine_part, latter * cosine + former * sine_part], axis=-1
    )


def query_rows(normed, q_weight, positions):
    mixed_rows = jnp.dot(normed, q_weight, preferred_element_type=jnp.float32)
    head_count = q_weight.shape[1] // (HN + HR)
    mixed_rows = mixed_rows.reshape(normed.shape[0], head_count, HN + HR)
    turned = rotate_pair(mixed_rows[:, :, HN:], angle_table(positions)[:, None, :])
    joined = jnp.concatenate([mixed_rows[:, :, :HN], turned], axis=2)
    return joined.reshape(normed.shape[0], head_count * (HN + HR)).astype(jnp.bfloat16)


def fresh_rows(normed, kv_down, latent_gain, positions):
    mixed_rows = jnp.dot(normed, kv_down, preferred_element_type=jnp.float32)
    latent = norm_rows(mixed_rows[:, :LAT], latent_gain)
    turned = rotate_pair(mixed_rows[:, LAT:], angle_table(positions))
    return jnp.concatenate([latent, turned], axis=1).astype(jnp.bfloat16)


def expand_rows(key_rows, kv_up):
    return jnp.dot(key_rows[:, :LAT], kv_up, preferred_element_type=jnp.float32).astype(
        jnp.bfloat16
    )


Q_BLOCK = 256


def attend_kernel(qn_ref, qr_ref, kw_ref, kr_ref, th_ref, o_ref):
    heads = qr_ref.shape[0]
    first = pl.program_id(0) * Q_BLOCK
    q_idx = first + lax.broadcasted_iota(jnp.int32, (Q_BLOCK, 1), 0)
    visible = q_idx >= th_ref[...]
    kr = kr_ref[...]
    contract = (((1,), (1,)), ((), ()))
    for h in range(heads):
        qn = qn_ref[:, h * HN : (h + 1) * HN]
        kn = kw_ref[:, h * (HN + HV) : h * (HN + HV) + HN]
        vals = kw_ref[:, h * (HN + HV) + HN : (h + 1) * (HN + HV)]
        scores = lax.dot_general(qn, kn, contract, preferred_element_type=jnp.float32)
        scores = scores + lax.dot_general(
            qr_ref[h], kr, contract, preferred_element_type=jnp.float32
        )
        scores = scores * (HN + HR) ** (-0.5)
        scores = jnp.where(visible, scores, -1e30)
        row_max = jnp.max(scores, axis=1, keepdims=True)
        weights = jnp.where(visible, jnp.exp(scores - row_max), 0.0)
        prob_rows = (weights / jnp.sum(weights, axis=1, keepdims=True)).astype(jnp.bfloat16)
        mixed = jnp.dot(prob_rows, vals, preferred_element_type=jnp.float32)
        o_ref[:, h * HV : (h + 1) * HV] = mixed.astype(jnp.bfloat16)


def attend_all(q_nope, q_rope, key_wide, rope_keys, thresh, interpret=False):
    span, nope_width = q_nope.shape
    heads = q_rope.shape[0]
    keys = key_wide.shape[0]
    return pl.pallas_call(
        attend_kernel,
        grid=(span // Q_BLOCK,),
        in_specs=[
            pl.BlockSpec((Q_BLOCK, nope_width), lambda i: (i, 0)),
            pl.BlockSpec((heads, Q_BLOCK, HR), lambda i: (0, i, 0)),
            pl.BlockSpec((keys, key_wide.shape[1]), lambda i: (0, 0)),
            pl.BlockSpec((keys, HR), lambda i: (0, 0)),
            pl.BlockSpec((1, keys), lambda i: (0, 0)),
        ],
        out_specs=pl.BlockSpec((Q_BLOCK, heads * HV), lambda i: (i, 0)),
        out_shape=jax.ShapeDtypeStruct((span, heads * HV), jnp.bfloat16),
        compiler_params=pltpu.CompilerParams(
            dimension_semantics=("arbitrary",), vmem_limit_bytes=48 * 1024 * 1024
        ),
        interpret=interpret,
    )(q_nope, q_rope, key_wide, rope_keys, thresh)


def expert_half(rows, gate_up, down):
    mixed_rows = jnp.dot(rows, gate_up, preferred_element_type=jnp.float32)
    active = (jax.nn.silu(mixed_rows[:, :HALF]) * mixed_rows[:, HALF:]).astype(jnp.bfloat16)
    return (
        jnp.dot(active, down, preferred_element_type=jnp.float32)
        .astype(jnp.bfloat16)
        .astype(jnp.float32)
    )


def layer_body(
    tokens,
    cached_lens,
    latent_cache,
    attn_gain,
    q_weight,
    kv_down,
    latent_gain,
    kv_up,
    o_weight,
    moe_gain,
    routes,
    route_weights,
    expert_gate_up,
    expert_down,
):
    head_count = lax.axis_size("z") * lax.axis_size("core")
    swap = [(0, 1), (1, 0)]
    other_gate_up = lax.ppermute(expert_gate_up, "core", swap)
    other_down = lax.ppermute(expert_down, "core", swap)
    request = lax.axis_index("dp")
    own_rows = tokens.shape[0]
    span_len = own_rows * head_count
    length = lax.dynamic_index_in_dim(cached_lens, request, 0, keepdims=False)
    local_heads = q_weight.shape[1] // (HN + HR)
    query_width = local_heads * (HN + HR)
    normed = norm_rows(tokens.astype(jnp.float32), attn_gain).astype(jnp.bfloat16)
    shard_rows = lax.all_gather(normed, HEAD, axis=0, tiled=True)
    o_src, shard_rows = lax.optimization_barrier((o_weight, shard_rows))
    o_full = lax.all_gather(o_src, HEAD, axis=0, tiled=True)
    positions = length + jnp.arange(shard_rows.shape[0], dtype=jnp.int32)
    projected = jnp.concatenate(
        [
            query_rows(shard_rows, q_weight, positions),
            fresh_rows(shard_rows, kv_down, latent_gain, positions),
        ],
        axis=1,
    )
    queries = projected[:, :query_width]
    fresh_keys = projected[:, query_width:]
    core = lax.axis_index("core")
    quarter = latent_cache.shape[1] // 2
    cache_part = lax.dynamic_slice_in_dim(latent_cache, core * quarter, quarter, 1)
    mine = lax.all_to_all(
        cache_part,
        "dp",
        split_axis=0,
        concat_axis=1,
        tiled=True,
    )[0]
    theirs = lax.ppermute(mine, "core", swap)
    cache_rows = jnp.arange(mine.shape[0], dtype=jnp.int32)
    cache_pos = cache_rows // quarter * (2 * quarter) + cache_rows % quarter
    key_rows = jnp.concatenate([mine, theirs, fresh_keys], axis=0)
    key_wide = expand_rows(key_rows, kv_up)
    rope_keys = key_rows[:, LAT:]
    key_index = jnp.concatenate(
        [
            cache_pos + core * quarter,
            cache_pos + (1 - core) * quarter,
            CACHE + jnp.arange(span_len, dtype=jnp.int32),
        ]
    )
    thresh = jnp.where(
        key_index < CACHE, jnp.where(key_index < length, -1, 1 << 30), key_index - CACHE
    ).reshape(1, -1)
    query_heads = queries.reshape(span_len, local_heads, HN + HR)
    heads_out = attend_all(
        query_heads[:, :, :HN].reshape(span_len, local_heads * HN),
        query_heads[:, :, HN:].transpose(1, 0, 2),
        key_wide,
        rope_keys,
        thresh,
    )
    heads_mine = lax.all_to_all(heads_out, HEAD, split_axis=0, concat_axis=1, tiled=True)
    group_terms = jnp.einsum(
        "tgc,gcd->gtd",
        heads_mine.reshape(own_rows, head_count, -1),
        o_full.reshape(head_count, -1, D),
        preferred_element_type=jnp.float32,
    )
    attn_out = jnp.sum(group_terms.astype(jnp.bfloat16).astype(jnp.float32), axis=0)
    hidden = tokens.astype(jnp.float32) + attn_out
    moe_in = norm_rows(hidden, moe_gain).astype(jnp.bfloat16)
    flat_routes = routes.reshape(-1)
    onehot = (flat_routes[:, None] == jnp.arange(EXPERTS, dtype=jnp.int32)[None, :]).astype(
        jnp.int32
    )
    rank_ids = jnp.sum((jnp.cumsum(onehot, axis=0) - onehot) * onehot, axis=1)
    slot_tk = (flat_routes * CAP + rank_ids).reshape(own_rows, TOPK)
    slot_iota = jnp.arange(EXPERTS * CAP, dtype=jnp.int32)
    dispatch = jnp.any(slot_tk[None, :, :] == slot_iota[:, None, None], axis=2).astype(
        jnp.bfloat16
    )
    outgoing = jnp.dot(dispatch, moe_in, preferred_element_type=jnp.float32).astype(jnp.bfloat16)
    arrived = lax.all_to_all(
        outgoing.reshape(EXPERTS, CAP, D), ("dp", "z"), split_axis=0, concat_axis=0, tiled=True
    ).reshape(EXPERTS * CAP, D)
    total = expert_half(arrived, expert_gate_up[0], expert_down[0]) + expert_half(
        arrived, other_gate_up[0], other_down[0]
    )
    returned = lax.all_to_all(
        total.astype(jnp.bfloat16).reshape(EXPERTS, CAP, D),
        ("dp", "z"),
        split_axis=0,
        concat_axis=0,
        tiled=True,
    ).reshape(EXPERTS * CAP, D)
    slot_weights = jnp.sum(
        jnp.where(slot_tk[:, :, None] == slot_iota[None, None, :], route_weights[:, :, None], 0.0),
        axis=1,
    )
    weights_hi = slot_weights.astype(jnp.bfloat16)
    weights_lo = (slot_weights - weights_hi.astype(jnp.float32)).astype(jnp.bfloat16)
    routed_out = jnp.dot(weights_hi, returned, preferred_element_type=jnp.float32) + jnp.dot(
        weights_lo, returned, preferred_element_type=jnp.float32
    )
    return (hidden + routed_out).astype(jnp.bfloat16)


def solution(mesh):
    chips = jax.sharding.Mesh(
        mesh.devices.reshape(mesh.shape["dp"], -1, 2), ("dp", "z", "core")
    )
    placed = (
        P(ROWS, None),
        P(),
        P(None, "dp", None),
        P(),
        P(None, HEAD),
        P(),
        P(),
        P(None, HEAD),
        P(HEAD, None),
        P(),
        P(ROWS, None),
        P(ROWS, None),
        P(ROWS, None, None),
        P(ROWS, None, None),
    )
    return jax.shard_map(
        layer_body, mesh=chips, in_specs=placed, out_specs=P(ROWS, None), check_vma=False
    )
```

```python
import jax
import jax.numpy as jnp
import numpy as np
from jax import lax
from jax.experimental import pallas as pl
from jax.experimental.pallas import tpu as pltpu
from jax.sharding import PartitionSpec as P

D = 2048
HN = 128
HR = 64
HV = 128
LAT = 512
EXPERTS = 64
TOPK = 6
CACHE = 2048
CAP = 16
HALF = 704
HEAD = ("z", "core")
ROWS = ("dp", "z", "core")


NORM_EPS = 1e-06


def norm_rows(values, gain_row):
    return (
        values * lax.rsqrt(jnp.mean(values * values, axis=-1, keepdims=True) + NORM_EPS) * gain_row
    )


def angle_table(positions):
    half_width = HR // 2
    inverse = np.exp(np.arange(half_width) * (-np.log(10000.0) / half_width)).astype(np.float32)
    return positions.astype(jnp.float32)[:, None] * jnp.asarray(inverse, dtype=jnp.float32)[None, :]


def rotate_pair(values, angles):
    half_width = values.shape[-1] // 2
    cosine = jnp.cos(angles)
    sine_part = jnp.sin(angles)
    former = values[..., :half_width]
    latter = values[..., half_width:]
    return jnp.concatenate(
        [former * cosine - latter * sine_part, latter * cosine + former * sine_part], axis=-1
    )


def query_rows(normed, q_weight, positions):
    mixed_rows = jnp.dot(normed, q_weight, preferred_element_type=jnp.float32)
    head_count = q_weight.shape[1] // (HN + HR)
    mixed_rows = mixed_rows.reshape(normed.shape[0], head_count, HN + HR)
    turned = rotate_pair(mixed_rows[:, :, HN:], angle_table(positions)[:, None, :])
    joined = jnp.concatenate([mixed_rows[:, :, :HN], turned], axis=2)
    return joined.reshape(normed.shape[0], head_count * (HN + HR)).astype(jnp.bfloat16)


def fresh_rows(normed, kv_down, latent_gain, positions):
    mixed_rows = jnp.dot(normed, kv_down, preferred_element_type=jnp.float32)
    latent = norm_rows(mixed_rows[:, :LAT], latent_gain)
    turned = rotate_pair(mixed_rows[:, LAT:], angle_table(positions))
    return jnp.concatenate([latent, turned], axis=1).astype(jnp.bfloat16)


def expand_rows(key_rows, kv_up):
    return jnp.dot(key_rows[:, :LAT], kv_up, preferred_element_type=jnp.float32).astype(
        jnp.bfloat16
    )


Q_BLOCK = 256


def attend_kernel(qn_ref, qr_ref, kw_ref, kr_ref, th_ref, o_ref):
    heads = qr_ref.shape[0]
    first = pl.program_id(0) * Q_BLOCK
    q_idx = first + lax.broadcasted_iota(jnp.int32, (Q_BLOCK, 1), 0)
    visible = q_idx >= th_ref[...]
    kr = kr_ref[...]
    contract = (((1,), (1,)), ((), ()))
    for h in range(heads):
        qn = qn_ref[:, h * HN : (h + 1) * HN]
        kn = kw_ref[:, h * (HN + HV) : h * (HN + HV) + HN]
        vals = kw_ref[:, h * (HN + HV) + HN : (h + 1) * (HN + HV)]
        scores = lax.dot_general(qn, kn, contract, preferred_element_type=jnp.float32)
        scores = scores + lax.dot_general(
            qr_ref[h], kr, contract, preferred_element_type=jnp.float32
        )
        scores = scores * (HN + HR) ** (-0.5)
        scores = jnp.where(visible, scores, -1e30)
        row_max = jnp.max(scores, axis=1, keepdims=True)
        weights = jnp.where(visible, jnp.exp(scores - row_max), 0.0)
        prob_rows = (weights / jnp.sum(weights, axis=1, keepdims=True)).astype(jnp.bfloat16)
        mixed = jnp.dot(prob_rows, vals, preferred_element_type=jnp.float32)
        o_ref[:, h * HV : (h + 1) * HV] = mixed.astype(jnp.bfloat16)


def attend_all(q_nope, q_rope, key_wide, rope_keys, thresh, interpret=False):
    span, nope_width = q_nope.shape
    heads = q_rope.shape[0]
    keys = key_wide.shape[0]
    return pl.pallas_call(
        attend_kernel,
        grid=(span // Q_BLOCK,),
        in_specs=[
            pl.BlockSpec((Q_BLOCK, nope_width), lambda i: (i, 0)),
            pl.BlockSpec((heads, Q_BLOCK, HR), lambda i: (0, i, 0)),
            pl.BlockSpec((keys, key_wide.shape[1]), lambda i: (0, 0)),
            pl.BlockSpec((keys, HR), lambda i: (0, 0)),
            pl.BlockSpec((1, keys), lambda i: (0, 0)),
        ],
        out_specs=pl.BlockSpec((Q_BLOCK, heads * HV), lambda i: (i, 0)),
        out_shape=jax.ShapeDtypeStruct((span, heads * HV), jnp.bfloat16),
        compiler_params=pltpu.CompilerParams(
            dimension_semantics=("arbitrary",), vmem_limit_bytes=48 * 1024 * 1024
        ),
        interpret=interpret,
    )(q_nope, q_rope, key_wide, rope_keys, thresh)


def expert_half(rows, gate_up, down):
    mixed_rows = jnp.dot(rows, gate_up, preferred_element_type=jnp.float32)
    active = (jax.nn.silu(mixed_rows[:, :HALF]) * mixed_rows[:, HALF:]).astype(jnp.bfloat16)
    return (
        jnp.dot(active, down, preferred_element_type=jnp.float32)
        .astype(jnp.bfloat16)
        .astype(jnp.float32)
    )


def layer_body(
    tokens,
    cached_lens,
    latent_cache,
    attn_gain,
    q_weight,
    kv_down,
    latent_gain,
    kv_up,
    o_weight,
    moe_gain,
    routes,
    route_weights,
    expert_gate_up,
    expert_down,
):
    head_count = lax.axis_size("z") * lax.axis_size("core")
    swap = [(0, 1), (1, 0)]
    other_gate_up = lax.ppermute(expert_gate_up, "core", swap)
    other_down = lax.ppermute(expert_down, "core", swap)
    request = lax.axis_index("dp")
    own_rows = tokens.shape[0]
    span_len = own_rows * head_count
    length = lax.dynamic_index_in_dim(cached_lens, request, 0, keepdims=False)
    local_heads = q_weight.shape[1] // (HN + HR)
    query_width = local_heads * (HN + HR)
    normed = norm_rows(tokens.astype(jnp.float32), attn_gain).astype(jnp.bfloat16)
    shard_rows = lax.all_gather(normed, HEAD, axis=0, tiled=True)
    o_src, shard_rows = lax.optimization_barrier((o_weight, shard_rows))
    o_full = lax.all_gather(o_src, HEAD, axis=0, tiled=True)
    positions = length + jnp.arange(shard_rows.shape[0], dtype=jnp.int32)
    projected = jnp.concatenate(
        [
            query_rows(shard_rows, q_weight, positions),
            fresh_rows(shard_rows, kv_down, latent_gain, positions),
        ],
        axis=1,
    )
    queries = projected[:, :query_width]
    fresh_keys = projected[:, query_width:]
    core = lax.axis_index("core")
    quarter = latent_cache.shape[1] // 2
    cache_part = lax.dynamic_slice_in_dim(latent_cache, core * quarter, quarter, 1)
    mine = lax.all_to_all(
        cache_part,
        "dp",
        split_axis=0,
        concat_axis=1,
        tiled=True,
    )[0]
    theirs = lax.ppermute(mine, "core", swap)
    cache_rows = jnp.arange(mine.shape[0], dtype=jnp.int32)
    cache_pos = cache_rows // quarter * (2 * quarter) + cache_rows % quarter
    key_rows = jnp.concatenate([mine, theirs, fresh_keys], axis=0)
    key_wide = expand_rows(key_rows, kv_up)
    rope_keys = key_rows[:, LAT:]
    key_index = jnp.concatenate(
        [
            cache_pos + core * quarter,
            cache_pos + (1 - core) * quarter,
            CACHE + jnp.arange(span_len, dtype=jnp.int32),
        ]
    )
    thresh = jnp.where(
        key_index < CACHE, jnp.where(key_index < length, -1, 1 << 30), key_index - CACHE
    ).reshape(1, -1)
    query_heads = queries.reshape(span_len, local_heads, HN + HR)
    heads_out = attend_all(
        query_heads[:, :, :HN].reshape(span_len, local_heads * HN),
        query_heads[:, :, HN:].transpose(1, 0, 2),
        key_wide,
        rope_keys,
        thresh,
    )
    heads_mine = lax.all_to_all(heads_out, HEAD, split_axis=0, concat_axis=1, tiled=True)
    group_terms = jnp.einsum(
        "tgc,gcd->gtd",
        heads_mine.reshape(own_rows, head_count, -1),
        o_full.reshape(head_count, -1, D),
        preferred_element_type=jnp.float32,
    )
    attn_out = jnp.sum(group_terms.astype(jnp.bfloat16).astype(jnp.float32), axis=0)
    hidden = tokens.astype(jnp.float32) + attn_out
    moe_in = norm_rows(hidden, moe_gain).astype(jnp.bfloat16)
    flat_routes = routes.reshape(-1)
    onehot = (flat_routes[:, None] == jnp.arange(EXPERTS, dtype=jnp.int32)[None, :]).astype(
        jnp.int32
    )
    rank_ids = jnp.sum((jnp.cumsum(onehot, axis=0) - onehot) * onehot, axis=1)
    slot_tk = (flat_routes * CAP + rank_ids).reshape(own_rows, TOPK)
    slot_iota = jnp.arange(EXPERTS * CAP, dtype=jnp.int32)
    dispatch = jnp.any(slot_tk[None, :, :] == slot_iota[:, None, None], axis=2).astype(
        jnp.bfloat16
    )
    outgoing = jnp.dot(dispatch, moe_in, preferred_element_type=jnp.float32).astype(jnp.bfloat16)
    outgoing = outgoing.reshape(EXPERTS, CAP, D)
    pieces = []
    for chunk in range(2):
        part = CAP // 2
        arrived = lax.all_to_all(
            outgoing[:, chunk * part : (chunk + 1) * part],
            ("dp", "z"),
            split_axis=0,
            concat_axis=0,
            tiled=True,
        ).reshape(EXPERTS * part, D)
        total = expert_half(arrived, expert_gate_up[0], expert_down[0]) + expert_half(
            arrived, other_gate_up[0], other_down[0]
        )
        pieces.append(
            lax.all_to_all(
                total.astype(jnp.bfloat16).reshape(EXPERTS, part, D),
                ("dp", "z"),
                split_axis=0,
                concat_axis=0,
                tiled=True,
            )
        )
    returned = jnp.concatenate(pieces, axis=1).reshape(EXPERTS * CAP, D)
    slot_weights = jnp.sum(
        jnp.where(slot_tk[:, :, None] == slot_iota[None, None, :], route_weights[:, :, None], 0.0),
        axis=1,
    )
    weights_hi = slot_weights.astype(jnp.bfloat16)
    weights_lo = (slot_weights - weights_hi.astype(jnp.float32)).astype(jnp.bfloat16)
    routed_out = jnp.dot(weights_hi, returned, preferred_element_type=jnp.float32) + jnp.dot(
        weights_lo, returned, preferred_element_type=jnp.float32
    )
    return (hidden + routed_out).astype(jnp.bfloat16)


def solution(mesh):
    chips = jax.sharding.Mesh(
        mesh.devices.reshape(mesh.shape["dp"], -1, 2), ("dp", "z", "core")
    )
    placed = (
        P(ROWS, None),
        P(),
        P(None, "dp", None),
        P(),
        P(None, HEAD),
        P(),
        P(),
        P(None, HEAD),
        P(HEAD, None),
        P(),
        P(ROWS, None),
        P(ROWS, None),
        P(ROWS, None, None),
        P(ROWS, None, None),
    )
    return jax.shard_map(
        layer_body, mesh=chips, in_specs=placed, out_specs=P(ROWS, None), check_vma=False
    )
```

```python
import jax
import jax.numpy as jnp
import numpy as np
from jax import lax
from jax.experimental import pallas as pl
from jax.experimental.pallas import tpu as pltpu
from jax.sharding import PartitionSpec as P

D = 2048
HN = 128
HR = 64
HV = 128
LAT = 512
EXPERTS = 64
TOPK = 6
CAP = 16
HALF = 704
HEAD = ("z", "core")
ROWS = ("dp", "z", "core")


NORM_EPS = 1e-06


def norm_rows(values, gain_row):
    return (
        values * lax.rsqrt(jnp.mean(values * values, axis=-1, keepdims=True) + NORM_EPS) * gain_row
    )


def angle_table(positions):
    half_width = HR // 2
    inverse = np.exp(np.arange(half_width) * (-np.log(10000.0) / half_width)).astype(np.float32)
    return positions.astype(jnp.float32)[:, None] * jnp.asarray(inverse, dtype=jnp.float32)[None, :]


def rotate_pair(values, angles):
    half_width = values.shape[-1] // 2
    cosine = jnp.cos(angles)
    sine_part = jnp.sin(angles)
    former = values[..., :half_width]
    latter = values[..., half_width:]
    return jnp.concatenate(
        [former * cosine - latter * sine_part, latter * cosine + former * sine_part], axis=-1
    )


def query_rows(normed, q_weight, positions):
    mixed_rows = jnp.dot(normed, q_weight, preferred_element_type=jnp.float32)
    head_count = q_weight.shape[1] // (HN + HR)
    mixed_rows = mixed_rows.reshape(normed.shape[0], head_count, HN + HR)
    turned = rotate_pair(mixed_rows[:, :, HN:], angle_table(positions)[:, None, :])
    joined = jnp.concatenate([mixed_rows[:, :, :HN], turned], axis=2)
    return joined.reshape(normed.shape[0], head_count * (HN + HR)).astype(jnp.bfloat16)


def expand_rows(key_rows, kv_up):
    return jnp.dot(key_rows[:, :LAT], kv_up, preferred_element_type=jnp.float32).astype(
        jnp.bfloat16
    )


Q_BLOCK = 512


def attend_kernel(qn_ref, qr_ref, *refs):
    o_ref = refs[-1]
    parts = [refs[i : i + 3] for i in range(0, len(refs) - 1, 3)]
    heads = qr_ref.shape[0]
    first = pl.program_id(0) * Q_BLOCK
    q_idx = first + lax.broadcasted_iota(jnp.int32, (Q_BLOCK, 1), 0)
    contract = (((1,), (1,)), ((), ()))
    for h in range(heads):
        qn = qn_ref[:, h * HN : (h + 1) * HN]
        qr = qr_ref[h]
        scores = []
        for kw_ref, kr_ref, th_ref in parts:
            kn = kw_ref[:, h * (HN + HV) : h * (HN + HV) + HN]
            part = lax.dot_general(qn, kn, contract, preferred_element_type=jnp.float32)
            part = part + lax.dot_general(
                qr, kr_ref[...], contract, preferred_element_type=jnp.float32
            )
            part = part * (HN + HR) ** (-0.5)
            scores.append(jnp.where(q_idx >= th_ref[...], part, -1e30))
        row_max = scores[0].max(axis=1, keepdims=True)
        for part in scores[1:]:
            row_max = jnp.maximum(row_max, part.max(axis=1, keepdims=True))
        weights = []
        for part, (kw_ref, kr_ref, th_ref) in zip(scores, parts):
            weights.append(jnp.where(q_idx >= th_ref[...], jnp.exp(part - row_max), 0.0))
        total = weights[0].sum(axis=1, keepdims=True)
        for part in weights[1:]:
            total = total + part.sum(axis=1, keepdims=True)
        mixed = jnp.zeros((Q_BLOCK, HV), jnp.float32)
        for part, (kw_ref, kr_ref, th_ref) in zip(weights, parts):
            vals = kw_ref[:, h * (HN + HV) + HN : (h + 1) * (HN + HV)]
            mixed = mixed + jnp.dot(
                (part / total).astype(jnp.bfloat16), vals, preferred_element_type=jnp.float32
            )
        o_ref[:, h * HV : (h + 1) * HV] = mixed.astype(jnp.bfloat16)


def attend_all(q_nope, q_rope, key_parts, interpret=False):
    span, nope_width = q_nope.shape
    heads = q_rope.shape[0]
    in_specs = [
        pl.BlockSpec((Q_BLOCK, nope_width), lambda i: (i, 0)),
        pl.BlockSpec((heads, Q_BLOCK, HR), lambda i: (0, i, 0)),
    ]
    operands = [q_nope, q_rope]
    for key_wide, rope_keys, thresh in key_parts:
        keys = key_wide.shape[0]
        in_specs += [
            pl.BlockSpec((keys, key_wide.shape[1]), lambda i: (0, 0)),
            pl.BlockSpec((keys, HR), lambda i: (0, 0)),
            pl.BlockSpec((1, keys), lambda i: (0, 0)),
        ]
        operands += [key_wide, rope_keys, thresh]
    return pl.pallas_call(
        attend_kernel,
        grid=(span // Q_BLOCK,),
        in_specs=in_specs,
        out_specs=pl.BlockSpec((Q_BLOCK, heads * HV), lambda i: (i, 0)),
        out_shape=jax.ShapeDtypeStruct((span, heads * HV), jnp.bfloat16),
        compiler_params=pltpu.CompilerParams(
            dimension_semantics=("arbitrary",), vmem_limit_bytes=48 * 1024 * 1024
        ),
        interpret=interpret,
    )(*operands)


def expert_half(rows, gate_up, down):
    mixed_rows = jnp.dot(rows, gate_up, preferred_element_type=jnp.float32)
    active = (jax.nn.silu(mixed_rows[:, :HALF]) * mixed_rows[:, HALF:]).astype(jnp.bfloat16)
    return (
        jnp.dot(active, down, preferred_element_type=jnp.float32)
        .astype(jnp.bfloat16)
        .astype(jnp.float32)
    )


def layer_body(
    tokens,
    cached_lens,
    latent_cache,
    attn_gain,
    q_weight,
    kv_down,
    latent_gain,
    kv_up,
    o_weight,
    moe_gain,
    routes,
    route_weights,
    expert_gate_up,
    expert_down,
):
    head_count = lax.axis_size("z") * lax.axis_size("core")
    swap = [(0, 1), (1, 0)]
    other_gate_up = lax.ppermute(expert_gate_up, "core", swap)
    other_down = lax.ppermute(expert_down, "core", swap)
    request = lax.axis_index("dp")
    own_rows = tokens.shape[0]
    span_len = own_rows * head_count
    length = lax.dynamic_index_in_dim(cached_lens, request, 0, keepdims=False)
    local_heads = q_weight.shape[1] // (HN + HR)
    normed = norm_rows(tokens.astype(jnp.float32), attn_gain).astype(jnp.bfloat16)
    shard_rows = lax.all_gather(normed, HEAD, axis=0, tiled=True)
    o_src, shard_rows = lax.optimization_barrier((o_weight, shard_rows))
    o_full = lax.all_gather(o_src, HEAD, axis=0, tiled=True)
    positions = length + jnp.arange(shard_rows.shape[0], dtype=jnp.int32)
    queries = query_rows(shard_rows, q_weight, positions)
    fresh_mixed = jnp.dot(shard_rows, kv_down, preferred_element_type=jnp.float32)
    fresh_latent = norm_rows(fresh_mixed[:, :LAT], latent_gain).astype(jnp.bfloat16)
    fresh_rope = rotate_pair(fresh_mixed[:, LAT:], angle_table(positions)).astype(jnp.bfloat16)
    core = lax.axis_index("core")
    quarter = latent_cache.shape[1] // 2
    cache_part = lax.dynamic_slice_in_dim(latent_cache, core * quarter, quarter, 1)
    mine = lax.all_to_all(
        cache_part,
        "dp",
        split_axis=0,
        concat_axis=1,
        tiled=True,
    )[0]
    theirs = lax.ppermute(mine, "core", swap)
    cache_rows = jnp.arange(mine.shape[0], dtype=jnp.int32)
    cache_pos = cache_rows // quarter * (2 * quarter) + cache_rows % quarter
    fresh_pos = jnp.arange(span_len, dtype=jnp.int32)

    def cache_thresh(pos):
        return jnp.where(pos < length, -1, 1 << 30).reshape(1, -1)

    key_parts = (
        (expand_rows(mine, kv_up), mine[:, LAT:], cache_thresh(cache_pos + core * quarter)),
        (
            expand_rows(theirs, kv_up),
            theirs[:, LAT:],
            cache_thresh(cache_pos + (1 - core) * quarter),
        ),
        (expand_rows(fresh_latent, kv_up), fresh_rope, fresh_pos.reshape(1, -1)),
    )
    query_heads = queries.reshape(span_len, local_heads, HN + HR)
    heads_out = attend_all(
        query_heads[:, :, :HN].reshape(span_len, local_heads * HN),
        query_heads[:, :, HN:].transpose(1, 0, 2),
        key_parts,
    )
    heads_mine = lax.all_to_all(heads_out, HEAD, split_axis=0, concat_axis=1, tiled=True)
    group_terms = jnp.einsum(
        "tgc,gcd->gtd",
        heads_mine.reshape(own_rows, head_count, -1),
        o_full.reshape(head_count, -1, D),
        preferred_element_type=jnp.float32,
    )
    attn_out = jnp.sum(group_terms.astype(jnp.bfloat16).astype(jnp.float32), axis=0)
    hidden = tokens.astype(jnp.float32) + attn_out
    moe_in = norm_rows(hidden, moe_gain).astype(jnp.bfloat16)
    flat_routes = routes.reshape(-1)
    onehot = (flat_routes[:, None] == jnp.arange(EXPERTS, dtype=jnp.int32)[None, :]).astype(
        jnp.int32
    )
    rank_ids = jnp.sum((jnp.cumsum(onehot, axis=0) - onehot) * onehot, axis=1)
    slot_tk = (flat_routes * CAP + rank_ids).reshape(own_rows, TOPK)
    slot_iota = jnp.arange(EXPERTS * CAP, dtype=jnp.int32)
    dispatch = jnp.any(slot_tk[None, :, :] == slot_iota[:, None, None], axis=2).astype(
        jnp.bfloat16
    )
    outgoing = jnp.dot(dispatch, moe_in, preferred_element_type=jnp.float32).astype(jnp.bfloat16)
    outgoing = outgoing.reshape(EXPERTS, CAP, D)
    pieces = []
    for chunk in range(2):
        part = CAP // 2
        arrived = lax.all_to_all(
            outgoing[:, chunk * part : (chunk + 1) * part],
            ("dp", "z"),
            split_axis=0,
            concat_axis=0,
            tiled=True,
        ).reshape(EXPERTS * part, D)
        total = expert_half(arrived, expert_gate_up[0], expert_down[0]) + expert_half(
            arrived, other_gate_up[0], other_down[0]
        )
        pieces.append(
            lax.all_to_all(
                total.astype(jnp.bfloat16).reshape(EXPERTS, part, D),
                ("dp", "z"),
                split_axis=0,
                concat_axis=0,
                tiled=True,
            )
        )
    returned = jnp.concatenate(pieces, axis=1).reshape(EXPERTS * CAP, D)
    slot_weights = jnp.sum(
        jnp.where(slot_tk[:, :, None] == slot_iota[None, None, :], route_weights[:, :, None], 0.0),
        axis=1,
    )
    weights_hi = slot_weights.astype(jnp.bfloat16)
    weights_lo = (slot_weights - weights_hi.astype(jnp.float32)).astype(jnp.bfloat16)
    routed_out = jnp.dot(weights_hi, returned, preferred_element_type=jnp.float32) + jnp.dot(
        weights_lo, returned, preferred_element_type=jnp.float32
    )
    return (hidden + routed_out).astype(jnp.bfloat16)


def solution(mesh):
    chips = jax.sharding.Mesh(
        mesh.devices.reshape(mesh.shape["dp"], -1, 2), ("dp", "z", "core")
    )
    placed = (
        P(ROWS, None),
        P(),
        P(None, "dp", None),
        P(),
        P(None, HEAD),
        P(),
        P(),
        P(None, HEAD),
        P(HEAD, None),
        P(),
        P(ROWS, None),
        P(ROWS, None),
        P(ROWS, None, None),
        P(ROWS, None, None),
    )
    return jax.shard_map(
        layer_body, mesh=chips, in_specs=placed, out_specs=P(ROWS, None), check_vma=False
    )
```

```python
import jax
import jax.numpy as jnp
import numpy as np
from jax import lax
from jax.experimental import pallas as pl
from jax.experimental.pallas import tpu as pltpu
from jax.sharding import PartitionSpec as P

D = 2048
HN = 128
HR = 64
HV = 128
LAT = 512
EXPERTS = 64
TOPK = 6
CAP = 16
HALF = 704
HEAD = ("z", "core")
ROWS = ("dp", "z", "core")


NORM_EPS = 1e-06


def norm_rows(values, gain_row):
    return (
        values * lax.rsqrt(jnp.mean(values * values, axis=-1, keepdims=True) + NORM_EPS) * gain_row
    )


def angle_table(positions):
    half_width = HR // 2
    inverse = np.exp(np.arange(half_width) * (-np.log(10000.0) / half_width)).astype(np.float32)
    return positions.astype(jnp.float32)[:, None] * jnp.asarray(inverse, dtype=jnp.float32)[None, :]


def rotate_pair(values, angles):
    half_width = values.shape[-1] // 2
    cosine = jnp.cos(angles)
    sine_part = jnp.sin(angles)
    former = values[..., :half_width]
    latter = values[..., half_width:]
    return jnp.concatenate(
        [former * cosine - latter * sine_part, latter * cosine + former * sine_part], axis=-1
    )


def query_rows(normed, q_weight, positions):
    mixed_rows = jnp.dot(normed, q_weight, preferred_element_type=jnp.float32)
    head_count = q_weight.shape[1] // (HN + HR)
    mixed_rows = mixed_rows.reshape(normed.shape[0], head_count, HN + HR)
    turned = rotate_pair(mixed_rows[:, :, HN:], angle_table(positions)[:, None, :])
    joined = jnp.concatenate([mixed_rows[:, :, :HN], turned], axis=2)
    return joined.reshape(normed.shape[0], head_count * (HN + HR)).astype(jnp.bfloat16)


def expand_rows(key_rows, kv_up):
    return jnp.dot(key_rows[:, :LAT], kv_up, preferred_element_type=jnp.float32).astype(
        jnp.bfloat16
    )


Q_BLOCK = 128


def attend_kernel(qn_ref, qr_ref, *refs):
    o_ref = refs[-1]
    parts = [refs[i : i + 3] for i in range(0, len(refs) - 1, 3)]
    heads = qr_ref.shape[0]
    first = pl.program_id(0) * Q_BLOCK
    q_idx = first + lax.broadcasted_iota(jnp.int32, (Q_BLOCK, 1), 0)
    contract = (((1,), (1,)), ((), ()))

    def one_head(h, carry):
        qn = qn_ref[:, pl.ds(pl.multiple_of(h * HN, HN), HN)]
        qr = qr_ref[h]
        scores = []
        for kw_ref, kr_ref, th_ref in parts:
            kn = kw_ref[:, pl.ds(pl.multiple_of(h * (HN + HV), HN + HV), HN)]
            part = lax.dot_general(qn, kn, contract, preferred_element_type=jnp.float32)
            part = part + lax.dot_general(
                qr, kr_ref[...], contract, preferred_element_type=jnp.float32
            )
            part = part * (HN + HR) ** (-0.5)
            scores.append(jnp.where(q_idx >= th_ref[...], part, -1e30))
        row_max = scores[0].max(axis=1, keepdims=True)
        for part in scores[1:]:
            row_max = jnp.maximum(row_max, part.max(axis=1, keepdims=True))
        weights = []
        for part, (kw_ref, kr_ref, th_ref) in zip(scores, parts):
            weights.append(jnp.where(q_idx >= th_ref[...], jnp.exp(part - row_max), 0.0))
        total = weights[0].sum(axis=1, keepdims=True)
        for part in weights[1:]:
            total = total + part.sum(axis=1, keepdims=True)
        mixed = jnp.zeros((Q_BLOCK, HV), jnp.float32)
        for part, (kw_ref, kr_ref, th_ref) in zip(weights, parts):
            vals = kw_ref[:, pl.ds(pl.multiple_of(h * (HN + HV) + HN, HN), HV)]
            mixed = mixed + jnp.dot(
                (part / total).astype(jnp.bfloat16), vals, preferred_element_type=jnp.float32
            )
        o_ref[:, pl.ds(pl.multiple_of(h * HV, HV), HV)] = mixed.astype(jnp.bfloat16)
        return carry

    lax.fori_loop(0, heads, one_head, 0)


def attend_all(q_nope, q_rope, key_parts, interpret=False):
    span, nope_width = q_nope.shape
    heads = q_rope.shape[0]
    in_specs = [
        pl.BlockSpec((Q_BLOCK, nope_width), lambda i: (i, 0)),
        pl.BlockSpec((heads, Q_BLOCK, HR), lambda i: (0, i, 0)),
    ]
    operands = [q_nope, q_rope]
    for key_wide, rope_keys, thresh in key_parts:
        keys = key_wide.shape[0]
        in_specs += [
            pl.BlockSpec((keys, key_wide.shape[1]), lambda i: (0, 0)),
            pl.BlockSpec((keys, HR), lambda i: (0, 0)),
            pl.BlockSpec((1, keys), lambda i: (0, 0)),
        ]
        operands += [key_wide, rope_keys, thresh]
    return pl.pallas_call(
        attend_kernel,
        grid=(span // Q_BLOCK,),
        in_specs=in_specs,
        out_specs=pl.BlockSpec((Q_BLOCK, heads * HV), lambda i: (i, 0)),
        out_shape=jax.ShapeDtypeStruct((span, heads * HV), jnp.bfloat16),
        compiler_params=pltpu.CompilerParams(
            dimension_semantics=("arbitrary",), vmem_limit_bytes=48 * 1024 * 1024
        ),
        interpret=interpret,
    )(*operands)


def expert_half(rows, gate_up, down):
    mixed_rows = jnp.dot(rows, gate_up, preferred_element_type=jnp.float32)
    active = (jax.nn.silu(mixed_rows[:, :HALF]) * mixed_rows[:, HALF:]).astype(jnp.bfloat16)
    return (
        jnp.dot(active, down, preferred_element_type=jnp.float32)
        .astype(jnp.bfloat16)
        .astype(jnp.float32)
    )


def layer_body(
    tokens,
    cached_lens,
    latent_cache,
    attn_gain,
    q_weight,
    kv_down,
    latent_gain,
    kv_up,
    o_weight,
    moe_gain,
    routes,
    route_weights,
    expert_gate_up,
    expert_down,
):
    head_count = lax.axis_size("z") * lax.axis_size("core")
    swap = [(0, 1), (1, 0)]
    other_gate_up = lax.ppermute(expert_gate_up, "core", swap)
    other_down = lax.ppermute(expert_down, "core", swap)
    request = lax.axis_index("dp")
    own_rows = tokens.shape[0]
    span_len = own_rows * head_count
    length = lax.dynamic_index_in_dim(cached_lens, request, 0, keepdims=False)
    local_heads = q_weight.shape[1] // (HN + HR)
    normed = norm_rows(tokens.astype(jnp.float32), attn_gain).astype(jnp.bfloat16)
    shard_rows = lax.all_gather(normed, HEAD, axis=0, tiled=True)
    o_src, shard_rows = lax.optimization_barrier((o_weight, shard_rows))
    o_full = lax.all_gather(o_src, HEAD, axis=0, tiled=True)
    positions = length + jnp.arange(shard_rows.shape[0], dtype=jnp.int32)
    queries = query_rows(shard_rows, q_weight, positions)
    fresh_mixed = jnp.dot(shard_rows, kv_down, preferred_element_type=jnp.float32)
    fresh_latent = norm_rows(fresh_mixed[:, :LAT], latent_gain).astype(jnp.bfloat16)
    fresh_rope = rotate_pair(fresh_mixed[:, LAT:], angle_table(positions)).astype(jnp.bfloat16)
    core = lax.axis_index("core")
    quarter = latent_cache.shape[1] // 2
    cache_part = lax.dynamic_slice_in_dim(latent_cache, core * quarter, quarter, 1)
    mine = lax.all_to_all(
        cache_part,
        "dp",
        split_axis=0,
        concat_axis=1,
        tiled=True,
    )[0]
    theirs = lax.ppermute(mine, "core", swap)
    cache_rows = jnp.arange(mine.shape[0], dtype=jnp.int32)
    cache_pos = cache_rows // quarter * (2 * quarter) + cache_rows % quarter
    fresh_pos = jnp.arange(span_len, dtype=jnp.int32)

    def cache_thresh(pos):
        return jnp.where(pos < length, -1, 1 << 30).reshape(1, -1)

    key_parts = (
        (expand_rows(mine, kv_up), mine[:, LAT:], cache_thresh(cache_pos + core * quarter)),
        (
            expand_rows(theirs, kv_up),
            theirs[:, LAT:],
            cache_thresh(cache_pos + (1 - core) * quarter),
        ),
        (expand_rows(fresh_latent, kv_up), fresh_rope, fresh_pos.reshape(1, -1)),
    )
    query_heads = queries.reshape(span_len, local_heads, HN + HR)
    heads_out = attend_all(
        query_heads[:, :, :HN].reshape(span_len, local_heads * HN),
        query_heads[:, :, HN:].transpose(1, 0, 2),
        key_parts,
    )
    heads_mine = lax.all_to_all(heads_out, HEAD, split_axis=0, concat_axis=1, tiled=True)
    group_terms = jnp.einsum(
        "tgc,gcd->gtd",
        heads_mine.reshape(own_rows, head_count, -1),
        o_full.reshape(head_count, -1, D),
        preferred_element_type=jnp.float32,
    )
    attn_out = jnp.sum(group_terms.astype(jnp.bfloat16).astype(jnp.float32), axis=0)
    hidden = tokens.astype(jnp.float32) + attn_out
    moe_in = norm_rows(hidden, moe_gain).astype(jnp.bfloat16)
    flat_routes = routes.reshape(-1)
    onehot = (flat_routes[:, None] == jnp.arange(EXPERTS, dtype=jnp.int32)[None, :]).astype(
        jnp.int32
    )
    rank_ids = jnp.sum((jnp.cumsum(onehot, axis=0) - onehot) * onehot, axis=1)
    slot_tk = (flat_routes * CAP + rank_ids).reshape(own_rows, TOPK)
    slot_iota = jnp.arange(EXPERTS * CAP, dtype=jnp.int32)
    dispatch = jnp.any(slot_tk[None, :, :] == slot_iota[:, None, None], axis=2).astype(
        jnp.bfloat16
    )
    outgoing = jnp.dot(dispatch, moe_in, preferred_element_type=jnp.float32).astype(jnp.bfloat16)
    outgoing = outgoing.reshape(EXPERTS, CAP, D)
    pieces = []
    for chunk in range(2):
        part = CAP // 2
        arrived = lax.all_to_all(
            outgoing[:, chunk * part : (chunk + 1) * part],
            ("dp", "z"),
            split_axis=0,
            concat_axis=0,
            tiled=True,
        ).reshape(EXPERTS * part, D)
        total = expert_half(arrived, expert_gate_up[0], expert_down[0]) + expert_half(
            arrived, other_gate_up[0], other_down[0]
        )
        pieces.append(
            lax.all_to_all(
                total.astype(jnp.bfloat16).reshape(EXPERTS, part, D),
                ("dp", "z"),
                split_axis=0,
                concat_axis=0,
                tiled=True,
            )
        )
    returned = jnp.concatenate(pieces, axis=1).reshape(EXPERTS * CAP, D)
    slot_weights = jnp.sum(
        jnp.where(slot_tk[:, :, None] == slot_iota[None, None, :], route_weights[:, :, None], 0.0),
        axis=1,
    )
    weights_hi = slot_weights.astype(jnp.bfloat16)
    weights_lo = (slot_weights - weights_hi.astype(jnp.float32)).astype(jnp.bfloat16)
    routed_out = jnp.dot(weights_hi, returned, preferred_element_type=jnp.float32) + jnp.dot(
        weights_lo, returned, preferred_element_type=jnp.float32
    )
    return (hidden + routed_out).astype(jnp.bfloat16)


def solution(mesh):
    chips = jax.sharding.Mesh(
        mesh.devices.reshape(mesh.shape["dp"], -1, 2), ("dp", "z", "core")
    )
    placed = (
        P(ROWS, None),
        P(),
        P(None, "dp", None),
        P(),
        P(None, HEAD),
        P(),
        P(),
        P(None, HEAD),
        P(HEAD, None),
        P(),
        P(ROWS, None),
        P(ROWS, None),
        P(ROWS, None, None),
        P(ROWS, None, None),
    )
    return jax.shard_map(
        layer_body, mesh=chips, in_specs=placed, out_specs=P(ROWS, None), check_vma=False
    )
```

```python
import jax
import jax.numpy as jnp
import numpy as np
from jax import lax
from jax.experimental import pallas as pl
from jax.experimental.pallas import tpu as pltpu
from jax.sharding import PartitionSpec as P

D = 2048
HN = 128
HR = 64
HV = 128
LAT = 512
EXPERTS = 64
TOPK = 6
CAP = 16
HALF = 704
HEAD = ("z", "core")
ROWS = ("dp", "z", "core")


NORM_EPS = 1e-06


def norm_rows(values, gain_row):
    return (
        values * lax.rsqrt(jnp.mean(values * values, axis=-1, keepdims=True) + NORM_EPS) * gain_row
    )


def angle_table(positions):
    half_width = HR // 2
    inverse = np.exp(np.arange(half_width) * (-np.log(10000.0) / half_width)).astype(np.float32)
    return positions.astype(jnp.float32)[:, None] * jnp.asarray(inverse, dtype=jnp.float32)[None, :]


def rotate_pair(values, angles):
    half_width = values.shape[-1] // 2
    cosine = jnp.cos(angles)
    sine_part = jnp.sin(angles)
    former = values[..., :half_width]
    latter = values[..., half_width:]
    return jnp.concatenate(
        [former * cosine - latter * sine_part, latter * cosine + former * sine_part], axis=-1
    )


def query_rows(normed, q_weight, positions):
    mixed_rows = jnp.dot(normed, q_weight, preferred_element_type=jnp.float32)
    head_count = q_weight.shape[1] // (HN + HR)
    mixed_rows = mixed_rows.reshape(normed.shape[0], head_count, HN + HR)
    turned = rotate_pair(mixed_rows[:, :, HN:], angle_table(positions)[:, None, :])
    joined = jnp.concatenate([mixed_rows[:, :, :HN], turned], axis=2)
    return joined.reshape(normed.shape[0], head_count * (HN + HR)).astype(jnp.bfloat16)


def expand_rows(key_rows, kv_up):
    return jnp.dot(key_rows[:, :LAT], kv_up, preferred_element_type=jnp.float32).astype(
        jnp.bfloat16
    )


Q_BLOCK = 256


def attend_kernel(qn_ref, qr_ref, *refs):
    o_ref = refs[-1]
    parts = [refs[i : i + 3] for i in range(0, len(refs) - 1, 3)]
    heads = qr_ref.shape[0]
    first = pl.program_id(0) * Q_BLOCK
    q_idx = first + lax.broadcasted_iota(jnp.int32, (Q_BLOCK, 1), 0)
    contract = (((1,), (1,)), ((), ()))

    def one_head(h, carry):
        qn = qn_ref[:, pl.ds(pl.multiple_of(h * HN, HN), HN)]
        qr = qr_ref[h]
        scores = []
        for kw_ref, kr_ref, th_ref in parts:
            kn = kw_ref[:, pl.ds(pl.multiple_of(h * (HN + HV), HN + HV), HN)]
            part = lax.dot_general(qn, kn, contract, preferred_element_type=jnp.float32)
            part = part + lax.dot_general(
                qr, kr_ref[...], contract, preferred_element_type=jnp.float32
            )
            part = part * (HN + HR) ** (-0.5)
            scores.append(jnp.where(q_idx >= th_ref[...], part, -1e30))
        row_max = scores[0].max(axis=1, keepdims=True)
        for part in scores[1:]:
            row_max = jnp.maximum(row_max, part.max(axis=1, keepdims=True))
        weights = []
        for part, (kw_ref, kr_ref, th_ref) in zip(scores, parts):
            weights.append(jnp.where(q_idx >= th_ref[...], jnp.exp(part - row_max), 0.0))
        total = weights[0].sum(axis=1, keepdims=True)
        for part in weights[1:]:
            total = total + part.sum(axis=1, keepdims=True)
        mixed = jnp.zeros((Q_BLOCK, HV), jnp.float32)
        for part, (kw_ref, kr_ref, th_ref) in zip(weights, parts):
            vals = kw_ref[:, pl.ds(pl.multiple_of(h * (HN + HV) + HN, HN), HV)]
            mixed = mixed + jnp.dot(
                (part / total).astype(jnp.bfloat16), vals, preferred_element_type=jnp.float32
            )
        o_ref[:, pl.ds(pl.multiple_of(h * HV, HV), HV)] = mixed.astype(jnp.bfloat16)
        return carry

    lax.fori_loop(0, heads, one_head, 0)


def attend_all(q_nope, q_rope, key_parts, interpret=False):
    span, nope_width = q_nope.shape
    heads = q_rope.shape[0]
    in_specs = [
        pl.BlockSpec((Q_BLOCK, nope_width), lambda i: (i, 0)),
        pl.BlockSpec((heads, Q_BLOCK, HR), lambda i: (0, i, 0)),
    ]
    operands = [q_nope, q_rope]
    for key_wide, rope_keys, thresh in key_parts:
        keys = key_wide.shape[0]
        in_specs += [
            pl.BlockSpec((keys, key_wide.shape[1]), lambda i: (0, 0)),
            pl.BlockSpec((keys, HR), lambda i: (0, 0)),
            pl.BlockSpec((1, keys), lambda i: (0, 0)),
        ]
        operands += [key_wide, rope_keys, thresh]
    return pl.pallas_call(
        attend_kernel,
        grid=(span // Q_BLOCK,),
        in_specs=in_specs,
        out_specs=pl.BlockSpec((Q_BLOCK, heads * HV), lambda i: (i, 0)),
        out_shape=jax.ShapeDtypeStruct((span, heads * HV), jnp.bfloat16),
        compiler_params=pltpu.CompilerParams(
            dimension_semantics=("arbitrary",), vmem_limit_bytes=48 * 1024 * 1024
        ),
        interpret=interpret,
    )(*operands)


def expert_half(rows, gate_up, down):
    mixed_rows = jnp.dot(rows, gate_up, preferred_element_type=jnp.float32)
    active = (jax.nn.silu(mixed_rows[:, :HALF]) * mixed_rows[:, HALF:]).astype(jnp.bfloat16)
    return (
        jnp.dot(active, down, preferred_element_type=jnp.float32)
        .astype(jnp.bfloat16)
        .astype(jnp.float32)
    )


def layer_body(
    tokens,
    cached_lens,
    latent_cache,
    attn_gain,
    q_weight,
    kv_down,
    latent_gain,
    kv_up,
    o_weight,
    moe_gain,
    routes,
    route_weights,
    expert_gate_up,
    expert_down,
):
    head_count = lax.axis_size("z") * lax.axis_size("core")
    swap = [(0, 1), (1, 0)]
    other_gate_up = lax.ppermute(expert_gate_up, "core", swap)
    other_down = lax.ppermute(expert_down, "core", swap)
    request = lax.axis_index("dp")
    own_rows = tokens.shape[0]
    span_len = own_rows * head_count
    length = lax.dynamic_index_in_dim(cached_lens, request, 0, keepdims=False)
    local_heads = q_weight.shape[1] // (HN + HR)
    normed = norm_rows(tokens.astype(jnp.float32), attn_gain).astype(jnp.bfloat16)
    shard_rows = lax.all_gather(normed, HEAD, axis=0, tiled=True)
    o_src, shard_rows = lax.optimization_barrier((o_weight, shard_rows))
    o_full = lax.all_gather(o_src, HEAD, axis=0, tiled=True)
    positions = length + jnp.arange(shard_rows.shape[0], dtype=jnp.int32)
    queries = query_rows(shard_rows, q_weight, positions)
    fresh_mixed = jnp.dot(shard_rows, kv_down, preferred_element_type=jnp.float32)
    fresh_latent = norm_rows(fresh_mixed[:, :LAT], latent_gain).astype(jnp.bfloat16)
    fresh_rope = rotate_pair(fresh_mixed[:, LAT:], angle_table(positions)).astype(jnp.bfloat16)
    core = lax.axis_index("core")
    quarter = latent_cache.shape[1] // 2
    cache_part = lax.dynamic_slice_in_dim(latent_cache, core * quarter, quarter, 1)
    mine = lax.all_to_all(
        cache_part,
        "dp",
        split_axis=0,
        concat_axis=1,
        tiled=True,
    )[0]
    theirs = lax.ppermute(mine, "core", swap)
    cache_rows = jnp.arange(mine.shape[0], dtype=jnp.int32)
    cache_pos = cache_rows // quarter * (2 * quarter) + cache_rows % quarter
    fresh_pos = jnp.arange(span_len, dtype=jnp.int32)

    def cache_thresh(pos):
        return jnp.where(pos < length, -1, 1 << 30).reshape(1, -1)

    key_parts = (
        (expand_rows(mine, kv_up), mine[:, LAT:], cache_thresh(cache_pos + core * quarter)),
        (
            expand_rows(theirs, kv_up),
            theirs[:, LAT:],
            cache_thresh(cache_pos + (1 - core) * quarter),
        ),
        (expand_rows(fresh_latent, kv_up), fresh_rope, fresh_pos.reshape(1, -1)),
    )
    query_heads = queries.reshape(span_len, local_heads, HN + HR)
    heads_out = attend_all(
        query_heads[:, :, :HN].reshape(span_len, local_heads * HN),
        query_heads[:, :, HN:].transpose(1, 0, 2),
        key_parts,
    )
    heads_mine = lax.all_to_all(heads_out, HEAD, split_axis=0, concat_axis=1, tiled=True)
    group_terms = jnp.einsum(
        "tgc,gcd->gtd",
        heads_mine.reshape(own_rows, head_count, -1),
        o_full.reshape(head_count, -1, D),
        preferred_element_type=jnp.float32,
    )
    attn_out = jnp.sum(group_terms.astype(jnp.bfloat16).astype(jnp.float32), axis=0)
    hidden = tokens.astype(jnp.float32) + attn_out
    moe_in = norm_rows(hidden, moe_gain).astype(jnp.bfloat16)
    flat_routes = routes.reshape(-1)
    onehot = (flat_routes[:, None] == jnp.arange(EXPERTS, dtype=jnp.int32)[None, :]).astype(
        jnp.int32
    )
    rank_ids = jnp.sum((jnp.cumsum(onehot, axis=0) - onehot) * onehot, axis=1)
    slot_tk = (flat_routes * CAP + rank_ids).reshape(own_rows, TOPK)
    slot_iota = jnp.arange(EXPERTS * CAP, dtype=jnp.int32)
    dispatch = jnp.any(slot_tk[None, :, :] == slot_iota[:, None, None], axis=2).astype(
        jnp.bfloat16
    )
    outgoing = jnp.dot(dispatch, moe_in, preferred_element_type=jnp.float32).astype(jnp.bfloat16)
    outgoing = outgoing.reshape(EXPERTS, CAP, D)
    pieces = []
    for chunk in range(2):
        part = CAP // 2
        arrived = lax.all_to_all(
            outgoing[:, chunk * part : (chunk + 1) * part],
            ("dp", "z"),
            split_axis=0,
            concat_axis=0,
            tiled=True,
        ).reshape(EXPERTS * part, D)
        total = expert_half(arrived, expert_gate_up[0], expert_down[0]) + expert_half(
            arrived, other_gate_up[0], other_down[0]
        )
        pieces.append(
            lax.all_to_all(
                total.astype(jnp.bfloat16).reshape(EXPERTS, part, D),
                ("dp", "z"),
                split_axis=0,
                concat_axis=0,
                tiled=True,
            )
        )
    returned = jnp.concatenate(pieces, axis=1).reshape(EXPERTS * CAP, D)
    slot_weights = jnp.sum(
        jnp.where(slot_tk[:, :, None] == slot_iota[None, None, :], route_weights[:, :, None], 0.0),
        axis=1,
    )
    weights_hi = slot_weights.astype(jnp.bfloat16)
    weights_lo = (slot_weights - weights_hi.astype(jnp.float32)).astype(jnp.bfloat16)
    both = jnp.dot(
        jnp.concatenate([weights_hi, weights_lo], axis=0),
        returned,
        preferred_element_type=jnp.float32,
    )
    routed_out = both[:own_rows] + both[own_rows:]
    return (hidden + routed_out).astype(jnp.bfloat16)


def solution(mesh):
    chips = jax.sharding.Mesh(
        mesh.devices.reshape(mesh.shape["dp"], -1, 2), ("dp", "z", "core")
    )
    placed = (
        P(ROWS, None),
        P(),
        P(None, "dp", None),
        P(),
        P(None, HEAD),
        P(),
        P(),
        P(None, HEAD),
        P(HEAD, None),
        P(),
        P(ROWS, None),
        P(ROWS, None),
        P(ROWS, None, None),
        P(ROWS, None, None),
    )
    return jax.shard_map(
        layer_body, mesh=chips, in_specs=placed, out_specs=P(ROWS, None), check_vma=False
    )
```
